32 devices in a mesh: blk: 8 (over y, x, core), xfer: 4 (over z).
Axes of the slice: x: 2, y: 2, z: 4, core: 2. Of those that a mesh axis runs over, the one named last changes fastest.
Arguments:
- greens: bfloat16 [8, 2, 256, 256], P('blk'), may hold values from -6 to 6
- transfer_index: int32 [64, 256], P(('blk', 'xfer')), may hold values from 0 to 255, as said below
- phase_index: int32 [64, 256], P(('blk', 'xfer')), may hold values from 0 to 7
- partner_slot: int32 [64], P(('blk', 'xfer')), may hold values from 0 to 1, as said below
- conj_index: int32 [256], replicated, may hold values from 0 to 255, as said below
Outputs:
- four_point: float32 [64, 2, 256, 256], P(('blk', 'xfer'))
The draws below stay inside these ranges and needn't reach their ends.
Inputs may be any that keep to these rules, and one draw needn't show every extreme that they name: `transfer_index`: each row is a permutation: the momentum-frequency shifted by the row's transfer, momenta on a periodic 4 x 4 cluster and frequencies cyclic over 16. `conj_index`: an involution: the index of the negated momentum and the mirrored frequency. `partner_slot`: the pairing is mutual: if transfer q in slot s has partner slot t on the partner device, the transfer in slot t there has partner slot s.
All inputs are finite; a program needn't handle non-finite values.
Results may differ from the reference program's by a relative error of at most 0.0003.
Values may be sent and summed in bfloat16 or wider, within the bound.
No kernel may reach another device: no remote copies, remote signals or barrier semaphores. Data moves between devices by JAX's collectives and lax.ppermute only.
A program may use at most 64 MiB of HBM per device.

```python
import math
import jax
import jax.numpy as jnp
from jax import lax

CSIDE = 4
NC = 16
NF = 16
NK = 256
NPH = 8
Q_DEV = 2
WALKERS = 8
NQ = 64
N_BLK = 8
N_XFER = 4


def labeling(key):
    return jax.random.permutation(jax.random.fold_in(key, 7), NK).astype(jnp.int32)


def coordinates():
    linear = jnp.arange(NK, dtype=jnp.int32)
    frequency = linear // NC
    cluster = linear % NC
    return (frequency, cluster // CSIDE, cluster % CSIDE)


def draw_conj_index(key, part):
    labels = labeling(key)
    frequency, column_x, column_y = coordinates()
    target = (NF - 1 - frequency) * NC + (CSIDE - column_x) % CSIDE * CSIDE + (CSIDE - column_y) % CSIDE
    return jnp.zeros((NK,), jnp.int32).at[labels].set(labels[target])


def draw_transfer_index(key, part):
    labels = labeling(key)
    frequency, column_x, column_y = coordinates()
    base = jax.random.fold_in(key, 11)
    shift_freq = jax.random.randint(jax.random.fold_in(base, 1), (NQ, 1), 0, NF)
    shift_x = jax.random.randint(jax.random.fold_in(base, 2), (NQ, 1), 0, CSIDE)
    shift_y = jax.random.randint(jax.random.fold_in(base, 3), (NQ, 1), 0, CSIDE)
    target = (frequency[None, :] + shift_freq) % NF * NC
    target = target + (column_x[None, :] + shift_x) % CSIDE * CSIDE + (column_y[None, :] + shift_y) % CSIDE
    return jnp.zeros((NQ, NK), jnp.int32).at[:, labels].set(labels[target])


def draw_partner_slot(key, part):
    halves = N_XFER // 2
    keys = jax.random.split(jax.random.fold_in(key, 13), N_BLK * halves)
    orders = jax.vmap(lambda single: jax.random.permutation(single, Q_DEV))(keys).astype(jnp.int32)
    inverse = jnp.argsort(orders, axis=-1, stable=True).astype(jnp.int32)
    orders = orders.reshape(N_BLK, halves, Q_DEV)
    inverse = inverse.reshape(N_BLK, halves, Q_DEV)
    return jnp.concatenate([orders, inverse], axis=1).reshape(NQ)


def set_ends(values, own_key, smallest, largest):
    shape = values.shape
    spot = [jax.random.randint(jax.random.fold_in(own_key, axis), (), 0, shape[axis]) for axis in range(len(shape))]
    values = values.at[tuple(spot)].set(smallest)
    longest = shape.index(max(shape))
    spot[longest] = (spot[longest] + 1) % shape[longest]
    return values.at[tuple(spot)].set(largest)


def shard_levels(rng, shape, cuts, smallest, top_value):
    factor_of = 1.0
    for axis_at, shards_of in cuts:
        steps = jax.random.uniform(jax.random.fold_in(jax.random.fold_in(rng, 6), axis_at), (shards_of,), jnp.float32, smallest / len(cuts), top_value / len(cuts))
        factor_of = factor_of * jnp.repeat(jnp.exp(steps), shape[axis_at] // shards_of).reshape((-1,) + (1,) * (len(shape) - 1 - axis_at))
    return factor_of


def normal_values(stream_key, shape, scale, most, shards=(), kind=jnp.bfloat16):
    gain = shard_levels(stream_key, shape, shards, -0.22, 0.18) if shards else 1.0
    drawn = jax.random.normal(stream_key, shape, jnp.float32) * scale * gain
    return jnp.minimum(jnp.maximum(drawn, -most), most).astype(kind)


def setup_inputs(seed: int = 0) -> dict:
    key_of = jax.random.split(jax.random.key(seed), 6)
    greens = normal_values(key_of[0], (WALKERS, 2, NK, NK), 1.0, 6.0, ((0, 8),))
    transfer_index = draw_transfer_index(jax.random.fold_in(key_of[5], 71), 0)
    phase_index = set_ends(jax.random.randint(key_of[2], (NQ, NK), 0, NPH), jax.random.fold_in(key_of[2], 1), 0, NPH - 1).astype(jnp.int32)
    partner_slot = draw_partner_slot(jax.random.fold_in(key_of[5], 71), 0)
    conj_index = draw_conj_index(jax.random.fold_in(key_of[5], 71), 0)
    return dict(greens=greens, transfer_index=transfer_index, phase_index=phase_index, partner_slot=partner_slot, conj_index=conj_index)


def reference(greens, transfer_index, phase_index, partner_slot, conj_index):

    def one_slice(pair):
        index_row, phase_row = pair

        def add_walker(total, block):
            values = block.astype(jnp.float32)
            moved = jnp.swapaxes(jnp.take(jnp.take(values, index_row, axis=1), index_row, axis=2), 1, 2)
            real = values[0] * moved[0] - values[1] * moved[1]
            imag = values[0] * moved[1] + values[1] * moved[0]
            return (total + jnp.stack([real, imag]), None)
        total = lax.scan(add_walker, jnp.zeros((2, NK, NK), jnp.float32), greens)[0]
        angle = 2.0 * math.pi / NPH * (phase_row[:, None] - phase_row[None, :]).astype(jnp.float32)
        cosines = jnp.cos(angle)
        sines = jnp.sin(angle)
        return jnp.stack([cosines * total[0] - sines * total[1], cosines * total[1] + sines * total[0]])
    sums = lax.map(one_slice, (transfer_index, phase_index))
    device = jnp.arange(NQ, dtype=jnp.int32) // Q_DEV
    row_group = device // N_XFER
    col_group = device % N_XFER
    partner = (row_group * N_XFER + (col_group + N_XFER // 2) % N_XFER) * Q_DEV + partner_slot

    def combine(which):
        mirror = sums[partner[which]]
        flipped = jnp.swapaxes(jnp.take(jnp.take(mirror, conj_index, axis=1), conj_index, axis=2), 1, 2)
        own = sums[which]
        return jnp.stack([own[0] + flipped[0], own[1] - flipped[1]]) * (0.5 / math.sqrt(WALKERS))
    return lax.map(combine, jnp.arange(NQ, dtype=jnp.int32))
```

```python
import math

import jax
import jax.numpy as jnp
from jax import lax
from jax.experimental import pallas as pl
from jax.experimental.pallas import tpu as pltpu
from jax.sharding import PartitionSpec as P

NPH = 8
F32 = jnp.float32
BF16 = jnp.bfloat16
NT = (((1,), (1,)), ((), ()))


def passed_along(value, axis, by):
    size = lax.axis_size(axis)
    return lax.ppermute(value, axis, [(i, (i + by) % size) for i in range(size)])


def one_hot(index_rows, width):
    columns = jnp.arange(width, dtype=jnp.int32)
    return (index_rows[..., :, None] == columns).astype(BF16)


def split3(x):
    hi = x.astype(BF16)
    r1 = x - hi.astype(F32)
    mid = r1.astype(BF16)
    lo = (r1 - mid.astype(F32)).astype(BF16)
    return (hi, mid, lo)


def conj_permuted(q, x):
    total = None
    for piece in split3(x):
        rows = jnp.dot(q, piece, preferred_element_type=F32).astype(BF16)
        moved = lax.dot_general(q, rows, NT, preferred_element_type=F32)
        total = moved if total is None else total + moved
    return total


def accumulate_kernel(g_ref, p_ref, q_ref, col_ref, row_ref, out_ref, acc_ref, *, slots, width, scale):
    w = pl.program_id(0)

    @pl.when(w == 0)
    def _():
        acc_ref[...] = jnp.zeros(acc_ref.shape, F32)

    g_re = g_ref[0, 0]
    g_im = g_ref[0, 1]
    sel = p_ref[...]
    y_re = jnp.dot(sel, g_re, preferred_element_type=F32).astype(BF16)
    y_im = jnp.dot(sel, g_im, preferred_element_type=F32).astype(BF16)
    gr = g_re.astype(F32)
    gi = g_im.astype(F32)
    for t in range(2 * slots):
        lo, hi = t * width, (t + 1) * width
        pt = sel[lo:hi]
        m_re = lax.dot_general(pt, y_re[lo:hi], NT, preferred_element_type=F32)
        m_im = lax.dot_general(pt, y_im[lo:hi], NT, preferred_element_type=F32)
        acc_ref[t, 0] += gr * m_re - gi * m_im
        acc_ref[t, 1] += gr * m_im + gi * m_re

    @pl.when(w == pl.num_programs(0) - 1)
    def _():
        q = q_ref[...]
        for s in range(slots):
            parts = []
            for t, permute in ((s, False), (s + slots, True)):
                t_re = acc_ref[t, 0]
                t_im = acc_ref[t, 1]
                if permute:
                    t_re = conj_permuted(q, t_re)
                    t_im = -conj_permuted(q, t_im)
                ca = col_ref[t, 0]
                sa = col_ref[t, 1]
                cb = row_ref[t, 0]
                sb = row_ref[t, 1]
                rot_re = ca * cb + sa * sb
                rot_im = sa * cb - ca * sb
                parts.append((rot_re * t_re - rot_im * t_im, rot_re * t_im + rot_im * t_re))
            (own_re, own_im), (mir_re, mir_im) = parts
            out_ref[s, 0] = (own_re + mir_re) * scale
            out_ref[s, 1] = (own_im + mir_im) * scale


def local(greens, transfer_index, phase_index, partner_slot, conj_index):
    slots = transfer_index.shape[0]
    width = greens.shape[-1]
    blocks = lax.axis_size("blk")
    halfway = lax.axis_size("xfer") // 2
    scale = 0.5 / math.sqrt(blocks)

    far_index = passed_along(transfer_index, "xfer", halfway)
    far_phase = passed_along(phase_index, "xfer", halfway)
    walkers = lax.all_gather(greens, "blk", axis=0, tiled=True)
    nwalk = walkers.shape[0]

    match_index = jnp.take(far_index, partner_slot, axis=0)
    match_phase = jnp.take(jnp.take(far_phase, partner_slot, axis=0), conj_index, axis=1)
    rows = jnp.concatenate([transfer_index, match_index], axis=0)
    sel = one_hot(rows, width).reshape(2 * slots * width, width)
    q = one_hot(conj_index, width)
    phases = jnp.concatenate([phase_index, match_phase], axis=0)
    angle = (2.0 * math.pi / NPH) * phases.astype(F32)
    trig = jnp.stack([jnp.cos(angle), jnp.sin(angle)], axis=1)
    col = trig[:, :, :, None]
    row = trig[:, :, None, :]

    kernel = lambda *refs: accumulate_kernel(*refs, slots=slots, width=width, scale=scale)
    full = lambda shape: pl.BlockSpec(shape, lambda w: (0,) * len(shape))
    return pl.pallas_call(
        kernel,
        grid=(nwalk,),
        in_specs=[
            pl.BlockSpec((1, 2, width, width), lambda w: (w, 0, 0, 0)),
            full(sel.shape),
            full(q.shape),
            full(col.shape),
            full(row.shape),
        ],
        out_specs=full((slots, 2, width, width)),
        out_shape=jax.ShapeDtypeStruct((slots, 2, width, width), F32),
        scratch_shapes=[pltpu.VMEM((2 * slots, 2, width, width), F32)],
        compiler_params=pltpu.CompilerParams(dimension_semantics=("arbitrary",)),
    )(walkers, sel, q, col, row)


def solution(mesh):
    in_specs = (
        P("blk", None, None, None),
        P(("blk", "xfer"), None),
        P(("blk", "xfer"), None),
        P(("blk", "xfer")),
        P(),
    )
    out_specs = P(("blk", "xfer"), None, None, None)
    return jax.shard_map(local, mesh=mesh, in_specs=in_specs, out_specs=out_specs, check_vma=False)
```

```python
import math

import jax
import jax.numpy as jnp
from jax import lax
from jax.experimental import pallas as pl
from jax.experimental.pallas import tpu as pltpu
from jax.sharding import PartitionSpec as P

NPH = 8
F32 = jnp.float32
BF16 = jnp.bfloat16
NT = (((1,), (1,)), ((), ()))


def passed_along(value, axis, by):
    size = lax.axis_size(axis)
    return lax.ppermute(value, axis, [(i, (i + by) % size) for i in range(size)])


def one_hot(index_rows, width):
    columns = jnp.arange(width, dtype=jnp.int32)
    return (index_rows[..., :, None] == columns).astype(BF16)


def split3(x):
    hi = x.astype(BF16)
    r1 = x - hi.astype(F32)
    mid = r1.astype(BF16)
    lo = (r1 - mid.astype(F32)).astype(BF16)
    return (hi, mid, lo)


def conj_permuted(q, x):
    total = None
    for piece in split3(x):
        rows = jnp.dot(q, piece, preferred_element_type=F32).astype(BF16)
        moved = lax.dot_general(q, rows, NT, preferred_element_type=F32)
        total = moved if total is None else total + moved
    return total


def add_walker(g_ref, p_ref, acc_ref, slots, width):
    g_re = g_ref[0, 0]
    g_im = g_ref[0, 1]
    sel = p_ref[...]
    y_re = jnp.dot(sel, g_re, preferred_element_type=F32).astype(BF16)
    y_im = jnp.dot(sel, g_im, preferred_element_type=F32).astype(BF16)
    gr = g_re.astype(F32)
    gi = g_im.astype(F32)
    for t in range(2 * slots):
        lo, hi = t * width, (t + 1) * width
        pt = sel[lo:hi]
        m_re = lax.dot_general(pt, y_re[lo:hi], NT, preferred_element_type=F32)
        m_im = lax.dot_general(pt, y_im[lo:hi], NT, preferred_element_type=F32)
        acc_ref[t, 0] += gr * m_re - gi * m_im
        acc_ref[t, 1] += gr * m_im + gi * m_re


def accumulate_kernel(near_ref, far_ref, p_ref, q_ref, col_ref, row_ref, out_ref, acc_ref, *, slots, width, scale, half):
    w = pl.program_id(0)

    @pl.when(w == 0)
    def _():
        acc_ref[...] = jnp.zeros(acc_ref.shape, F32)

    @pl.when(w < half)
    def _():
        add_walker(near_ref, p_ref, acc_ref, slots, width)

    @pl.when(w >= half)
    def _():
        add_walker(far_ref, p_ref, acc_ref, slots, width)

    @pl.when(w == pl.num_programs(0) - 1)
    def _():
        q = q_ref[...]
        for s in range(slots):
            parts = []
            for t, permute in ((s, False), (s + slots, True)):
                t_re = acc_ref[t, 0]
                t_im = acc_ref[t, 1]
                if permute:
                    t_re = conj_permuted(q, t_re)
                    t_im = -conj_permuted(q, t_im)
                ca = col_ref[t, 0]
                sa = col_ref[t, 1]
                cb = row_ref[t, 0]
                sb = row_ref[t, 1]
                rot_re = ca * cb + sa * sb
                rot_im = sa * cb - ca * sb
                parts.append((rot_re * t_re - rot_im * t_im, rot_re * t_im + rot_im * t_re))
            (own_re, own_im), (mir_re, mir_im) = parts
            out_ref[s, 0] = (own_re + mir_re) * scale
            out_ref[s, 1] = (own_im + mir_im) * scale


def local(greens, transfer_index, phase_index, partner_slot, conj_index):
    slots = transfer_index.shape[0]
    width = greens.shape[-1]
    blocks = lax.axis_size("blk")
    halfway = lax.axis_size("xfer") // 2
    scale = 0.5 / math.sqrt(blocks)

    far_index = passed_along(transfer_index, "xfer", halfway)
    far_phase = passed_along(phase_index, "xfer", halfway)
    half = blocks // 2
    assert blocks % 2 == 0 and blocks & (blocks - 1) == 0
    fetched = [greens]
    for m in range(1, half):
        fetched.append(lax.ppermute(greens, "blk", [(i, i ^ (2 * m)) for i in range(blocks)]))
    near = jnp.concatenate(fetched, axis=0)
    sibling = lax.ppermute(near, "blk", [(i, i ^ 1) for i in range(blocks)])
    nwalk = 2 * half

    match_index = jnp.take(far_index, partner_slot, axis=0)
    match_phase = jnp.take(jnp.take(far_phase, partner_slot, axis=0), conj_index, axis=1)
    rows = jnp.concatenate([transfer_index, match_index], axis=0)
    sel = one_hot(rows, width).reshape(2 * slots * width, width)
    q = one_hot(conj_index, width)
    phases = jnp.concatenate([phase_index, match_phase], axis=0)
    angle = (2.0 * math.pi / NPH) * phases.astype(F32)
    trig = jnp.stack([jnp.cos(angle), jnp.sin(angle)], axis=1)
    col = trig[:, :, :, None]
    row = trig[:, :, None, :]

    kernel = lambda *refs: accumulate_kernel(*refs, slots=slots, width=width, scale=scale, half=half)
    full = lambda shape: pl.BlockSpec(shape, lambda w: (0,) * len(shape))
    return pl.pallas_call(
        kernel,
        grid=(nwalk,),
        in_specs=[
            pl.BlockSpec((1, 2, width, width), lambda w: (jnp.minimum(w, half - 1), 0, 0, 0)),
            pl.BlockSpec((1, 2, width, width), lambda w: (jnp.maximum(w - half, 0), 0, 0, 0)),
            full(sel.shape),
            full(q.shape),
            full(col.shape),
            full(row.shape),
        ],
        out_specs=full((slots, 2, width, width)),
        out_shape=jax.ShapeDtypeStruct((slots, 2, width, width), F32),
        scratch_shapes=[pltpu.VMEM((2 * slots, 2, width, width), F32)],
        compiler_params=pltpu.CompilerParams(dimension_semantics=("arbitrary",)),
    )(near, sibling, sel, q, col, row)


def solution(mesh):
    in_specs = (
        P("blk", None, None, None),
        P(("blk", "xfer"), None),
        P(("blk", "xfer"), None),
        P(("blk", "xfer")),
        P(),
    )
    out_specs = P(("blk", "xfer"), None, None, None)
    return jax.shard_map(local, mesh=mesh, in_specs=in_specs, out_specs=out_specs, check_vma=False)
```

```python
import functools
import math

import jax
import jax.numpy as jnp
from jax import lax
from jax.experimental import pallas as pl
from jax.experimental.pallas import tpu as pltpu
from jax.sharding import PartitionSpec as P

NPH = 8
F32 = jnp.float32
BF16 = jnp.bfloat16
NT = (((1,), (1,)), ((), ()))


def passed_along(value, axis, by):
    size = lax.axis_size(axis)
    return lax.ppermute(value, axis, [(i, (i + by) % size) for i in range(size)])


def one_hot(index_rows, width):
    columns = jnp.arange(width, dtype=jnp.int32)
    return (index_rows[..., :, None] == columns).astype(BF16)


def split3(x):
    hi = x.astype(BF16)
    r1 = x - hi.astype(F32)
    mid = r1.astype(BF16)
    lo = (r1 - mid.astype(F32)).astype(BF16)
    return (hi, mid, lo)


def conj_permuted(q, x):
    total = None
    for piece in split3(x):
        rows = jnp.dot(q, piece, preferred_element_type=F32).astype(BF16)
        moved = lax.dot_general(q, rows, NT, preferred_element_type=F32)
        total = moved if total is None else total + moved
    return total


def add_walker(g_ref, p_ref, acc_ref, slots, width):
    g_re = g_ref[0, 0]
    g_im = g_ref[0, 1]
    sel = p_ref[...]
    y_re = jnp.dot(sel, g_re, preferred_element_type=F32).astype(BF16)
    y_im = jnp.dot(sel, g_im, preferred_element_type=F32).astype(BF16)
    gr = g_re.astype(F32)
    gi = g_im.astype(F32)
    for t in range(2 * slots):
        lo, hi = t * width, (t + 1) * width
        pt = sel[lo:hi]
        m_re = lax.dot_general(pt, y_re[lo:hi], NT, preferred_element_type=F32)
        m_im = lax.dot_general(pt, y_im[lo:hi], NT, preferred_element_type=F32)
        acc_ref[t, 0] += gr * m_re - gi * m_im
        acc_ref[t, 1] += gr * m_im + gi * m_re


def accumulate_kernel(*refs, slots, width, scale, has_prior, final):
    if has_prior:
        g_ref, p_ref, q_ref, col_ref, row_ref, prior_hbm, out_ref, acc_ref, prior_ref, sem = refs
    else:
        g_ref, p_ref, q_ref, col_ref, row_ref, out_ref, acc_ref = refs
    w = pl.program_id(0)
    last = pl.num_programs(0) - 1

    @pl.when(w == 0)
    def _():
        acc_ref[...] = jnp.zeros(acc_ref.shape, F32)
        if has_prior:
            pltpu.make_async_copy(prior_hbm, prior_ref, sem).start()

    add_walker(g_ref, p_ref, acc_ref, slots, width)

    @pl.when(w == last)
    def _():
        if has_prior:
            pltpu.make_async_copy(prior_hbm, prior_ref, sem).wait()
        if not final:
            if has_prior:
                out_ref[...] = acc_ref[...] + prior_ref[...]
            else:
                out_ref[...] = acc_ref[...]
            return
        q = q_ref[...]
        for s in range(slots):
            parts = []
            for t, permute in ((s, False), (s + slots, True)):
                t_re = acc_ref[t, 0] + prior_ref[t, 0]
                t_im = acc_ref[t, 1] + prior_ref[t, 1]
                if permute:
                    t_re = conj_permuted(q, t_re)
                    t_im = -conj_permuted(q, t_im)
                ca = col_ref[t, 0]
                sa = col_ref[t, 1]
                cb = row_ref[t, 0]
                sb = row_ref[t, 1]
                rot_re = ca * cb + sa * sb
                rot_im = sa * cb - ca * sb
                parts.append((rot_re * t_re - rot_im * t_im, rot_re * t_im + rot_im * t_re))
            (own_re, own_im), (mir_re, mir_im) = parts
            out_ref[s, 0] = (own_re + mir_re) * scale
            out_ref[s, 1] = (own_im + mir_im) * scale


def accumulate(walkers, sel, q, col, row, prior, final, slots, width, scale):
    has_prior = prior is not None
    kernel = functools.partial(
        accumulate_kernel, slots=slots, width=width, scale=scale, has_prior=has_prior, final=final
    )
    full = lambda shape: pl.BlockSpec(shape, lambda w: (0,) * len(shape))
    acc_shape = (2 * slots, 2, width, width)
    out_shape = (slots, 2, width, width) if final else acc_shape
    in_specs = [
        pl.BlockSpec((1, 2, width, width), lambda w: (w, 0, 0, 0)),
        full(sel.shape),
        full(q.shape),
        full(col.shape),
        full(row.shape),
    ]
    scratch = [pltpu.VMEM(acc_shape, F32)]
    operands = [walkers, sel, q, col, row]
    if has_prior:
        in_specs.append(pl.BlockSpec(memory_space=pl.ANY))
        scratch += [pltpu.VMEM(acc_shape, F32), pltpu.SemaphoreType.DMA(())]
        operands.append(prior)
    steps = walkers.shape[0]
    flops = steps * 2 * slots * 8 * width**3 + (12 * slots * 2 * width**3 if final else 0)
    moved = walkers.size * 2 + sel.size * 2 + 4 * math.prod(out_shape) + (4 * math.prod(acc_shape) if has_prior else 0)
    return pl.pallas_call(
        kernel,
        grid=(steps,),
        cost_estimate=pl.CostEstimate(flops=flops, transcendentals=0, bytes_accessed=moved),
        in_specs=in_specs,
        out_specs=full(out_shape),
        out_shape=jax.ShapeDtypeStruct(out_shape, F32),
        scratch_shapes=scratch,
        compiler_params=pltpu.CompilerParams(dimension_semantics=("arbitrary",)),
    )(*operands)


def local(greens, transfer_index, phase_index, partner_slot, conj_index):
    slots = transfer_index.shape[0]
    width = greens.shape[-1]
    blocks = lax.axis_size("blk")
    halfway = lax.axis_size("xfer") // 2
    scale = 0.5 / math.sqrt(blocks)
    assert blocks % 2 == 0 and blocks & (blocks - 1) == 0

    far_index = passed_along(transfer_index, "xfer", halfway)
    far_phase = passed_along(phase_index, "xfer", halfway)
    swap = [(i, i ^ 1) for i in range(blocks)]
    sibling = lax.ppermute(greens, "blk", swap)
    fetched = [lax.ppermute(greens, "blk", [(i, i ^ (2 * m)) for i in range(blocks)]) for m in range(1, blocks // 2)]

    match_index = jnp.take(far_index, partner_slot, axis=0)
    match_phase = jnp.take(jnp.take(far_phase, partner_slot, axis=0), conj_index, axis=1)
    rows = jnp.concatenate([transfer_index, match_index], axis=0)
    sel = one_hot(rows, width).reshape(2 * slots * width, width)
    q = one_hot(conj_index, width)
    phases = jnp.concatenate([phase_index, match_phase], axis=0)
    angle = (2.0 * math.pi / NPH) * phases.astype(F32)
    trig = jnp.stack([jnp.cos(angle), jnp.sin(angle)], axis=1)
    col = trig[:, :, :, None]
    row = trig[:, :, None, :]
    run = functools.partial(accumulate, sel=sel, q=q, col=col, row=row, slots=slots, width=width, scale=scale)

    if not fetched:
        return run(jnp.concatenate([greens, sibling], axis=0), prior=None, final=True)
    partial_sums = run(jnp.concatenate([greens, sibling], axis=0), prior=None, final=False)
    partial_sums, fetched = lax.optimization_barrier((partial_sums, fetched))
    near = jnp.concatenate(fetched, axis=0)
    forwarded = lax.ppermute(near, "blk", swap)
    partial_sums = run(near, prior=partial_sums, final=False)
    return run(forwarded, prior=partial_sums, final=True)


def solution(mesh):
    in_specs = (
        P("blk", None, None, None),
        P(("blk", "xfer"), None),
        P(("blk", "xfer"), None),
        P(("blk", "xfer")),
        P(),
    )
    out_specs = P(("blk", "xfer"), None, None, None)
    return jax.shard_map(local, mesh=mesh, in_specs=in_specs, out_specs=out_specs, check_vma=False)
```

```python
import functools
import math

import jax
import jax.numpy as jnp
from jax import lax
from jax.experimental import pallas as pl
from jax.experimental.pallas import tpu as pltpu
from jax.sharding import PartitionSpec as P

NPH = 8
F32 = jnp.float32
BF16 = jnp.bfloat16
NT = (((1,), (1,)), ((), ()))


def passed_along(value, axis, by):
    size = lax.axis_size(axis)
    return lax.ppermute(value, axis, [(i, (i + by) % size) for i in range(size)])


def one_hot(index_rows, width):
    columns = jnp.arange(width, dtype=jnp.int32)
    return (index_rows[..., :, None] == columns).astype(BF16)


def split3(x):
    hi = x.astype(BF16)
    r1 = x - hi.astype(F32)
    mid = r1.astype(BF16)
    lo = (r1 - mid.astype(F32)).astype(BF16)
    return (hi, mid, lo)


def conj_permuted(q, x):
    total = None
    for piece in split3(x):
        rows = jnp.dot(q, piece, preferred_element_type=F32).astype(BF16)
        moved = lax.dot_general(q, rows, NT, preferred_element_type=F32)
        total = moved if total is None else total + moved
    return total


def add_walker(g_ref, p_ref, acc_ref, slots, width):
    g_re = g_ref[0, 0]
    g_im = g_ref[0, 1]
    sel = p_ref[...]
    y_re = jnp.dot(sel, g_re, preferred_element_type=F32).astype(BF16)
    y_im = jnp.dot(sel, g_im, preferred_element_type=F32).astype(BF16)
    gr = g_re.astype(F32)
    gi = g_im.astype(F32)
    for t in range(2 * slots):
        lo, hi = t * width, (t + 1) * width
        pt = sel[lo:hi]
        m_re = lax.dot_general(pt, y_re[lo:hi], NT, preferred_element_type=F32)
        m_im = lax.dot_general(pt, y_im[lo:hi], NT, preferred_element_type=F32)
        acc_ref[t, 0] += gr * m_re - gi * m_im
        acc_ref[t, 1] += gr * m_im + gi * m_re


def accumulate_kernel(*refs, slots, width, scale, has_prior, final):
    if has_prior:
        g_ref, p_ref, q_ref, col_ref, row_ref, prior_hbm, out_ref, acc_ref, prior_ref, sem = refs
    else:
        g_ref, p_ref, q_ref, col_ref, row_ref, out_ref, acc_ref = refs
    w = pl.program_id(0)
    last = pl.num_programs(0) - 1

    @pl.when(w == 0)
    def _():
        acc_ref[...] = jnp.zeros(acc_ref.shape, F32)
        if has_prior:
            pltpu.make_async_copy(prior_hbm, prior_ref, sem).start()

    add_walker(g_ref, p_ref, acc_ref, slots, width)

    @pl.when(w == last)
    def _():
        if has_prior:
            pltpu.make_async_copy(prior_hbm, prior_ref, sem).wait()
        if not final:
            if has_prior:
                out_ref[...] = acc_ref[...] + prior_ref[...]
            else:
                out_ref[...] = acc_ref[...]
            return
        q = q_ref[...]
        for s in range(slots):
            parts = []
            for t, permute in ((s, False), (s + slots, True)):
                t_re = acc_ref[t, 0] + prior_ref[t, 0]
                t_im = acc_ref[t, 1] + prior_ref[t, 1]
                if permute:
                    t_re = conj_permuted(q, t_re)
                    t_im = -conj_permuted(q, t_im)
                ca = col_ref[t, 0]
                sa = col_ref[t, 1]
                cb = row_ref[t, 0]
                sb = row_ref[t, 1]
                rot_re = ca * cb + sa * sb
                rot_im = sa * cb - ca * sb
                parts.append((rot_re * t_re - rot_im * t_im, rot_re * t_im + rot_im * t_re))
            (own_re, own_im), (mir_re, mir_im) = parts
            out_ref[s, 0] = (own_re + mir_re) * scale
            out_ref[s, 1] = (own_im + mir_im) * scale


def accumulate(walkers, sel, q, col, row, prior, final, slots, width, scale):
    has_prior = prior is not None
    kernel = functools.partial(
        accumulate_kernel, slots=slots, width=width, scale=scale, has_prior=has_prior, final=final
    )
    full = lambda shape: pl.BlockSpec(shape, lambda w: (0,) * len(shape))
    acc_shape = (2 * slots, 2, width, width)
    out_shape = (slots, 2, width, width) if final else acc_shape
    in_specs = [
        pl.BlockSpec((1, 2, width, width), lambda w: (w, 0, 0, 0)),
        full(sel.shape),
        full(q.shape),
        full(col.shape),
        full(row.shape),
    ]
    scratch = [pltpu.VMEM(acc_shape, F32)]
    operands = [walkers, sel, q, col, row]
    if has_prior:
        in_specs.append(pl.BlockSpec(memory_space=pl.ANY))
        scratch += [pltpu.VMEM(acc_shape, F32), pltpu.SemaphoreType.DMA(())]
        operands.append(prior)
    steps = walkers.shape[0]
    flops = steps * 2 * slots * 8 * width**3 + (12 * slots * 2 * width**3 if final else 0)
    moved = walkers.size * 2 + sel.size * 2 + 4 * math.prod(out_shape) + (4 * math.prod(acc_shape) if has_prior else 0)
    return pl.pallas_call(
        kernel,
        grid=(steps,),
        cost_estimate=pl.CostEstimate(flops=flops, transcendentals=0, bytes_accessed=moved),
        in_specs=in_specs,
        out_specs=full(out_shape),
        out_shape=jax.ShapeDtypeStruct(out_shape, F32),
        scratch_shapes=scratch,
        compiler_params=pltpu.CompilerParams(dimension_semantics=("arbitrary",)),
    )(*operands)


def local(greens, transfer_index, phase_index, partner_slot, conj_index):
    slots = transfer_index.shape[0]
    width = greens.shape[-1]
    blocks = lax.axis_size("blk")
    halfway = lax.axis_size("xfer") // 2
    scale = 0.5 / math.sqrt(blocks)
    assert blocks % 2 == 0 and blocks & (blocks - 1) == 0

    far_index = passed_along(transfer_index, "xfer", halfway)
    far_phase = passed_along(phase_index, "xfer", halfway)
    swap = [(i, i ^ 1) for i in range(blocks)]
    sibling = lax.ppermute(greens, "blk", swap)
    fetched = [lax.ppermute(greens, "blk", [(i, i ^ (2 * m)) for i in range(blocks)]) for m in range(1, blocks // 2)]

    match_index = jnp.take(far_index, partner_slot, axis=0)
    match_phase = jnp.take(jnp.take(far_phase, partner_slot, axis=0), conj_index, axis=1)
    rows = jnp.concatenate([transfer_index, match_index], axis=0)
    sel = one_hot(rows, width).reshape(2 * slots * width, width)
    q = one_hot(conj_index, width)
    phases = jnp.concatenate([phase_index, match_phase], axis=0)
    angle = (2.0 * math.pi / NPH) * phases.astype(F32)
    trig = jnp.stack([jnp.cos(angle), jnp.sin(angle)], axis=1)
    col = trig[:, :, :, None]
    row = trig[:, :, None, :]
    run = functools.partial(accumulate, sel=sel, q=q, col=col, row=row, slots=slots, width=width, scale=scale)

    if not fetched:
        return run(jnp.concatenate([greens, sibling], axis=0), prior=None, final=True)
    near = jnp.concatenate(fetched, axis=0)
    forwarded = lax.ppermute(near, "blk", swap)
    partial_sums = run(jnp.concatenate([greens, sibling, near], axis=0), prior=None, final=False)
    return run(forwarded, prior=partial_sums, final=True)


def solution(mesh):
    in_specs = (
        P("blk", None, None, None),
        P(("blk", "xfer"), None),
        P(("blk", "xfer"), None),
        P(("blk", "xfer")),
        P(),
    )
    out_specs = P(("blk", "xfer"), None, None, None)
    return jax.shard_map(local, mesh=mesh, in_specs=in_specs, out_specs=out_specs, check_vma=False)
```

```python
import functools
import math

import jax
import jax.numpy as jnp
from jax import lax
from jax.experimental import pallas as pl
from jax.experimental.pallas import tpu as pltpu
from jax.sharding import PartitionSpec as P

NPH = 8
F32 = jnp.float32
BF16 = jnp.bfloat16
NT = (((1,), (1,)), ((), ()))
ROOT_HALF = math.sqrt(0.5)
COSINES = (1.0, ROOT_HALF, 0.0, -ROOT_HALF, -1.0, -ROOT_HALF, 0.0, ROOT_HALF)
SINES = (0.0, ROOT_HALF, 1.0, ROOT_HALF, 0.0, -ROOT_HALF, -1.0, -ROOT_HALF)


def passed_along(value, axis, by):
    size = lax.axis_size(axis)
    return lax.ppermute(value, axis, [(i, (i + by) % size) for i in range(size)])


def split3(x):
    hi = x.astype(BF16)
    r1 = x - hi.astype(F32)
    mid = r1.astype(BF16)
    lo = (r1 - mid.astype(F32)).astype(BF16)
    return (hi, mid, lo)


def conj_permuted(q, x):
    total = None
    for piece in split3(x):
        rows = jnp.dot(q, piece, preferred_element_type=F32).astype(BF16)
        moved = lax.dot_general(q, rows, NT, preferred_element_type=F32)
        total = moved if total is None else total + moved
    return total


def table(levels, values):
    out = jnp.zeros(levels.shape, F32)
    for k, v in enumerate(values):
        out = jnp.where(levels == k, v, out)
    return out


def add_walker(g_ref, sel_ref, acc_ref, slots, width):
    g_re = g_ref[0, 0]
    g_im = g_ref[0, 1]
    sel = sel_ref[...]
    y_re = jnp.dot(sel, g_re, preferred_element_type=F32).astype(BF16)
    y_im = jnp.dot(sel, g_im, preferred_element_type=F32).astype(BF16)
    gr = g_re.astype(F32)
    gi = g_im.astype(F32)
    for t in range(2 * slots):
        lo, hi = t * width, (t + 1) * width
        pt = sel[lo:hi]
        m_re = lax.dot_general(pt, y_re[lo:hi], NT, preferred_element_type=F32)
        m_im = lax.dot_general(pt, y_im[lo:hi], NT, preferred_element_type=F32)
        acc_ref[t, 0] += gr * m_re - gi * m_im
        acc_ref[t, 1] += gr * m_im + gi * m_re


def accumulate_kernel(*refs, slots, width, scale, has_prior, final):
    if has_prior:
        (g_ref, ti_ref, ph_ref, far_ref, slot_ref, cj_ref, prior_hbm, out_ref,
         acc_ref, sel_ref, prior_ref, sem) = refs
    else:
        g_ref, ti_ref, ph_ref, far_ref, slot_ref, cj_ref, out_ref, acc_ref, sel_ref = refs
    w = pl.program_id(0)
    last = pl.num_programs(0) - 1
    nt = 2 * slots
    lanes = lax.broadcasted_iota(jnp.int32, (width, width), 1).astype(F32)

    def columns():
        far = far_ref[...]
        rows = [ti_ref[pl.ds(s, 1), :] for s in range(slots)]
        for s in range(slots):
            pick = slot_ref[s]
            rows.append(jnp.where(pick == 0, far[0:1], far[1:2]))
        rows.append(cj_ref[...])
        block = jnp.concatenate(rows, axis=0).astype(F32)
        block = jnp.concatenate([block, jnp.zeros((128 - block.shape[0], width), F32)], axis=0)
        return block.T

    @pl.when(w == 0)
    def _():
        acc_ref[...] = jnp.zeros(acc_ref.shape, F32)
        if has_prior:
            pltpu.make_async_copy(prior_hbm, prior_ref, sem).start()
        cols = columns()
        for t in range(nt):
            sel_ref[t * width:(t + 1) * width] = (cols[:, t:t + 1] == lanes).astype(BF16)

    add_walker(g_ref, sel_ref, acc_ref, slots, width)

    @pl.when(w == last)
    def _():
        if has_prior:
            pltpu.make_async_copy(prior_hbm, prior_ref, sem).wait()
        if not final:
            if has_prior:
                out_ref[...] = acc_ref[...] + prior_ref[...]
            else:
                out_ref[...] = acc_ref[...]
            return
        cols = columns()
        q = (cols[:, nt:nt + 1] == lanes).astype(BF16)
        far = far_ref[...]
        partner = [jnp.where(slot_ref[s] == 0, far[2:3], far[3:4]) for s in range(slots)]
        partner = jnp.concatenate(partner + [jnp.zeros((8 - slots, width), jnp.int32)], axis=0)
        partner = lax.dot_general(partner.astype(F32).astype(BF16), q, NT, preferred_element_type=F32)
        levels = jnp.concatenate([ph_ref[...].astype(F32), partner[:slots]], axis=0)
        trig = jnp.concatenate([table(levels, COSINES), table(levels, SINES)], axis=0)
        trig_cols = jnp.concatenate([trig, jnp.zeros((128 - 2 * nt, width), F32)], axis=0).T
        for s in range(slots):
            parts = []
            for t, permute in ((s, False), (s + slots, True)):
                t_re = acc_ref[t, 0] + prior_ref[t, 0] if has_prior else acc_ref[t, 0]
                t_im = acc_ref[t, 1] + prior_ref[t, 1] if has_prior else acc_ref[t, 1]
                if permute:
                    t_re = conj_permuted(q, t_re)
                    t_im = -conj_permuted(q, t_im)
                ca = trig_cols[:, t:t + 1]
                sa = trig_cols[:, nt + t:nt + t + 1]
                cb = trig[t:t + 1]
                sb = trig[nt + t:nt + t + 1]
                rot_re = ca * cb + sa * sb
                rot_im = sa * cb - ca * sb
                parts.append((rot_re * t_re - rot_im * t_im, rot_re * t_im + rot_im * t_re))
            (own_re, own_im), (mir_re, mir_im) = parts
            out_ref[s, 0] = (own_re + mir_re) * scale
            out_ref[s, 1] = (own_im + mir_im) * scale


def accumulate(walkers, info, prior, final, slots, width, scale):
    has_prior = prior is not None
    kernel = functools.partial(
        accumulate_kernel, slots=slots, width=width, scale=scale, has_prior=has_prior, final=final
    )
    full = lambda shape: pl.BlockSpec(shape, lambda w: (0,) * len(shape))
    acc_shape = (2 * slots, 2, width, width)
    out_shape = (slots, 2, width, width) if final else acc_shape
    ti, ph, far, slot, cj = info
    in_specs = [
        pl.BlockSpec((1, 2, width, width), lambda w: (w, 0, 0, 0)),
        full(ti.shape),
        full(ph.shape),
        full(far.shape),
        pl.BlockSpec(memory_space=pltpu.SMEM),
        full(cj.shape),
    ]
    scratch = [pltpu.VMEM(acc_shape, F32), pltpu.VMEM((2 * slots * width, width), BF16)]
    operands = [walkers, ti, ph, far, slot, cj]
    if has_prior:
        in_specs.append(pl.BlockSpec(memory_space=pl.ANY))
        scratch += [pltpu.VMEM(acc_shape, F32), pltpu.SemaphoreType.DMA(())]
        operands.append(prior)
    steps = walkers.shape[0]
    flops = steps * 2 * slots * 8 * width**3 + (12 * slots * 2 * width**3 if final else 0)
    moved = walkers.size * 2 + 4 * math.prod(out_shape) + (4 * math.prod(acc_shape) if has_prior else 0)
    return pl.pallas_call(
        kernel,
        grid=(steps,),
        cost_estimate=pl.CostEstimate(flops=flops, transcendentals=0, bytes_accessed=moved),
        in_specs=in_specs,
        out_specs=full(out_shape),
        out_shape=jax.ShapeDtypeStruct(out_shape, F32),
        scratch_shapes=scratch,
        compiler_params=pltpu.CompilerParams(dimension_semantics=("arbitrary",)),
    )(*operands)


def local(greens, transfer_index, phase_index, partner_slot, conj_index):
    slots = transfer_index.shape[0]
    width = greens.shape[-1]
    blocks = lax.axis_size("blk")
    halfway = lax.axis_size("xfer") // 2
    scale = 0.5 / math.sqrt(blocks)
    assert blocks % 2 == 0 and blocks & (blocks - 1) == 0 and 4 * slots + 1 <= 128

    swap = [(i, i ^ 1) for i in range(blocks)]
    sibling = lax.ppermute(greens, "blk", swap)
    fetched = [lax.ppermute(greens, "blk", [(i, i ^ (2 * m)) for i in range(blocks)]) for m in range(1, blocks // 2)]
    far = passed_along(jnp.concatenate([transfer_index, phase_index], axis=0), "xfer", halfway)
    info = (transfer_index, phase_index, far, partner_slot, conj_index.reshape(1, width))
    run = functools.partial(accumulate, info=info, slots=slots, width=width, scale=scale)

    if not fetched:
        return run(jnp.concatenate([greens, sibling], axis=0), prior=None, final=True)
    near = jnp.concatenate(fetched, axis=0)
    forwarded = lax.ppermute(near, "blk", swap)
    partial_sums = run(jnp.concatenate([greens, sibling, near], axis=0), prior=None, final=False)
    return run(forwarded, prior=partial_sums, final=True)


def solution(mesh):
    in_specs = (
        P("blk", None, None, None),
        P(("blk", "xfer"), None),
        P(("blk", "xfer"), None),
        P(("blk", "xfer")),
        P(),
    )
    out_specs = P(("blk", "xfer"), None, None, None)
    return jax.shard_map(local, mesh=mesh, in_specs=in_specs, out_specs=out_specs, check_vma=False)
```

```python
import functools
import math

import jax
import jax.numpy as jnp
from jax import lax
from jax.experimental import pallas as pl
from jax.experimental.pallas import tpu as pltpu
from jax.sharding import PartitionSpec as P

NPH = 8
F32 = jnp.float32
BF16 = jnp.bfloat16
NT = (((1,), (1,)), ((), ()))
ROOT_HALF = math.sqrt(0.5)
COSINES = (1.0, ROOT_HALF, 0.0, -ROOT_HALF, -1.0, -ROOT_HALF, 0.0, ROOT_HALF)
SINES = (0.0, ROOT_HALF, 1.0, ROOT_HALF, 0.0, -ROOT_HALF, -1.0, -ROOT_HALF)


def passed_along(value, axis, by):
    size = lax.axis_size(axis)
    return lax.ppermute(value, axis, [(i, (i + by) % size) for i in range(size)])


def split3(x):
    hi = x.astype(BF16)
    r1 = x - hi.astype(F32)
    mid = r1.astype(BF16)
    lo = (r1 - mid.astype(F32)).astype(BF16)
    return (hi, mid, lo)


def conj_permuted(q, x):
    total = None
    for piece in split3(x):
        rows = jnp.dot(q, piece, preferred_element_type=F32).astype(BF16)
        moved = lax.dot_general(q, rows, NT, preferred_element_type=F32)
        total = moved if total is None else total + moved
    return total


def table(levels, values):
    out = jnp.zeros(levels.shape, F32)
    for k, v in enumerate(values):
        out = jnp.where(levels == k, v, out)
    return out


def add_walker(g_ref, sel_ref, acc_ref, slots, width):
    g_re = g_ref[0, 0]
    g_im = g_ref[0, 1]
    sel = sel_ref[...]
    y_re = jnp.dot(sel, g_re, preferred_element_type=F32).astype(BF16)
    y_im = jnp.dot(sel, g_im, preferred_element_type=F32).astype(BF16)
    gr = g_re.astype(F32)
    gi = g_im.astype(F32)
    for t in range(2 * slots):
        lo, hi = t * width, (t + 1) * width
        pt = sel[lo:hi]
        m_re = lax.dot_general(pt, y_re[lo:hi], NT, preferred_element_type=F32)
        m_im = lax.dot_general(pt, y_im[lo:hi], NT, preferred_element_type=F32)
        acc_ref[t, 0] += gr * m_re - gi * m_im
        acc_ref[t, 1] += gr * m_im + gi * m_re


def accumulate_kernel(*refs, slots, width, scale, has_prior, final):
    if has_prior:
        (g_ref, ti_ref, ph_ref, far_ref, slot_ref, cj_ref, prior_hbm, out_ref,
         acc_ref, sel_ref, prior_ref, sem) = refs
    else:
        g_ref, ti_ref, ph_ref, far_ref, slot_ref, cj_ref, out_ref, acc_ref, sel_ref = refs
    w = pl.program_id(0)
    last = pl.num_programs(0) - 1
    nt = 2 * slots
    lanes = lax.broadcasted_iota(jnp.int32, (width, width), 1).astype(F32)

    def columns():
        far = far_ref[...]
        rows = [ti_ref[pl.ds(s, 1), :] for s in range(slots)]
        for s in range(slots):
            pick = slot_ref[s]
            rows.append(jnp.where(pick == 0, far[0:1], far[1:2]))
        rows.append(cj_ref[...])
        block = jnp.concatenate(rows, axis=0).astype(F32)
        block = jnp.concatenate([block, jnp.zeros((128 - block.shape[0], width), F32)], axis=0)
        return block.T

    @pl.when(w == 0)
    def _():
        acc_ref[...] = jnp.zeros(acc_ref.shape, F32)
        if has_prior:
            pltpu.make_async_copy(prior_hbm, prior_ref, sem).start()
        cols = columns()
        for t in range(nt):
            sel_ref[t * width:(t + 1) * width] = (cols[:, t:t + 1] == lanes).astype(BF16)

    add_walker(g_ref, sel_ref, acc_ref, slots, width)

    @pl.when(w == last)
    def _():
        if has_prior:
            pltpu.make_async_copy(prior_hbm, prior_ref, sem).wait()
        if not final:
            if has_prior:
                out_ref[...] = acc_ref[...] + prior_ref[...]
            else:
                out_ref[...] = acc_ref[...]
            return
        cols = columns()
        q = (cols[:, nt:nt + 1] == lanes).astype(BF16)
        far = far_ref[...]
        partner = [jnp.where(slot_ref[s] == 0, far[2:3], far[3:4]) for s in range(slots)]
        partner = jnp.concatenate(partner + [jnp.zeros((8 - slots, width), jnp.int32)], axis=0)
        partner = lax.dot_general(partner.astype(F32).astype(BF16), q, NT, preferred_element_type=F32)
        levels = jnp.concatenate([ph_ref[...].astype(F32), partner[:slots]], axis=0)
        trig = jnp.concatenate([table(levels, COSINES), table(levels, SINES)], axis=0)
        trig_cols = jnp.concatenate([trig, jnp.zeros((128 - 2 * nt, width), F32)], axis=0).T
        for s in range(slots):
            parts = []
            for t, permute in ((s, False), (s + slots, True)):
                t_re = acc_ref[t, 0] + prior_ref[t, 0] if has_prior else acc_ref[t, 0]
                t_im = acc_ref[t, 1] + prior_ref[t, 1] if has_prior else acc_ref[t, 1]
                if permute:
                    t_re = conj_permuted(q, t_re)
                    t_im = -conj_permuted(q, t_im)
                ca = trig_cols[:, t:t + 1]
                sa = trig_cols[:, nt + t:nt + t + 1]
                cb = trig[t:t + 1]
                sb = trig[nt + t:nt + t + 1]
                rot_re = ca * cb + sa * sb
                rot_im = sa * cb - ca * sb
                parts.append((rot_re * t_re - rot_im * t_im, rot_re * t_im + rot_im * t_re))
            (own_re, own_im), (mir_re, mir_im) = parts
            out_ref[s, 0] = (own_re + mir_re) * scale
            out_ref[s, 1] = (own_im + mir_im) * scale


def accumulate(walkers, info, prior, final, slots, width, scale):
    has_prior = prior is not None
    kernel = functools.partial(
        accumulate_kernel, slots=slots, width=width, scale=scale, has_prior=has_prior, final=final
    )
    full = lambda shape: pl.BlockSpec(shape, lambda w: (0,) * len(shape))
    acc_shape = (2 * slots, 2, width, width)
    out_shape = (slots, 2, width, width) if final else acc_shape
    ti, ph, far, slot, cj = info
    in_specs = [
        pl.BlockSpec((1, 2, width, width), lambda w: (w, 0, 0, 0)),
        full(ti.shape),
        full(ph.shape),
        full(far.shape),
        pl.BlockSpec(memory_space=pltpu.SMEM),
        full(cj.shape),
    ]
    scratch = [pltpu.VMEM(acc_shape, F32), pltpu.VMEM((2 * slots * width, width), BF16)]
    operands = [walkers, ti, ph, far, slot, cj]
    if has_prior:
        in_specs.append(pl.BlockSpec(memory_space=pl.ANY))
        scratch += [pltpu.VMEM(acc_shape, F32), pltpu.SemaphoreType.DMA(())]
        operands.append(prior)
    steps = walkers.shape[0]
    flops = steps * 2 * slots * 8 * width**3 + (12 * slots * 2 * width**3 if final else 0)
    moved = walkers.size * 2 + 4 * math.prod(out_shape) + (4 * math.prod(acc_shape) if has_prior else 0)
    return pl.pallas_call(
        kernel,
        grid=(steps,),
        cost_estimate=pl.CostEstimate(flops=flops, transcendentals=0, bytes_accessed=moved),
        in_specs=in_specs,
        out_specs=full(out_shape),
        out_shape=jax.ShapeDtypeStruct(out_shape, F32),
        scratch_shapes=scratch,
        compiler_params=pltpu.CompilerParams(dimension_semantics=("arbitrary",)),
    )(*operands)


def local(greens, transfer_index, phase_index, partner_slot, conj_index):
    slots = transfer_index.shape[0]
    width = greens.shape[-1]
    blocks = lax.axis_size("blk")
    halfway = lax.axis_size("xfer") // 2
    scale = 0.5 / math.sqrt(blocks)
    assert blocks % 2 == 0 and blocks & (blocks - 1) == 0 and 4 * slots + 1 <= 128

    swap = [(i, i ^ 1) for i in range(blocks)]
    sibling = lax.ppermute(greens, "blk", swap)
    fetched = [lax.ppermute(greens, "blk", [(i, i ^ (2 * m)) for i in range(blocks)]) for m in range(1, blocks // 2)]
    far = passed_along(jnp.concatenate([transfer_index, phase_index], axis=0), "xfer", halfway)
    info = (transfer_index, phase_index, far, partner_slot, conj_index.reshape(1, width))
    run = functools.partial(accumulate, info=info, slots=slots, width=width, scale=scale)

    if not fetched:
        return run(jnp.concatenate([greens, sibling], axis=0), prior=None, final=True)
    partial_sums = run(jnp.concatenate([greens, sibling], axis=0), prior=None, final=False)
    partial_sums, fetched = lax.optimization_barrier((partial_sums, fetched))
    near = jnp.concatenate(fetched, axis=0)
    forwarded = lax.ppermute(near, "blk", swap)
    partial_sums = run(near, prior=partial_sums, final=False)
    return run(forwarded, prior=partial_sums, final=True)


def solution(mesh):
    in_specs = (
        P("blk", None, None, None),
        P(("blk", "xfer"), None),
        P(("blk", "xfer"), None),
        P(("blk", "xfer")),
        P(),
    )
    out_specs = P(("blk", "xfer"), None, None, None)
    return jax.shard_map(local, mesh=mesh, in_specs=in_specs, out_specs=out_specs, check_vma=False)
```

```python
import functools
import math

import jax
import jax.numpy as jnp
from jax import lax
from jax.experimental import pallas as pl
from jax.experimental.pallas import tpu as pltpu
from jax.sharding import PartitionSpec as P

NPH = 8
F32 = jnp.float32
BF16 = jnp.bfloat16
NT = (((1,), (1,)), ((), ()))
ROOT_HALF = math.sqrt(0.5)
COSINES = (1.0, ROOT_HALF, 0.0, -ROOT_HALF, -1.0, -ROOT_HALF, 0.0, ROOT_HALF)
SINES = (0.0, ROOT_HALF, 1.0, ROOT_HALF, 0.0, -ROOT_HALF, -1.0, -ROOT_HALF)


def passed_along(value, axis, by):
    size = lax.axis_size(axis)
    return lax.ppermute(value, axis, [(i, (i + by) % size) for i in range(size)])


def split3(x):
    hi = x.astype(BF16)
    r1 = x - hi.astype(F32)
    mid = r1.astype(BF16)
    lo = (r1 - mid.astype(F32)).astype(BF16)
    return (hi, mid, lo)


def conj_permuted(q, x):
    total = None
    for piece in split3(x):
        rows = jnp.dot(q, piece, preferred_element_type=F32).astype(BF16)
        moved = lax.dot_general(q, rows, NT, preferred_element_type=F32)
        total = moved if total is None else total + moved
    return total


def table(levels, values):
    out = jnp.zeros(levels.shape, F32)
    for k, v in enumerate(values):
        out = jnp.where(levels == k, v, out)
    return out


def add_walker(g_ref, sel_ref, acc_ref, slots, width):
    g_re = g_ref[0, 0]
    g_im = g_ref[0, 1]
    sel = sel_ref[...]
    y = jnp.dot(sel, jnp.concatenate([g_re, g_im], axis=1), preferred_element_type=F32).astype(BF16)
    gr = g_re.astype(F32)
    gi = g_im.astype(F32)
    for t in range(2 * slots):
        lo, hi = t * width, (t + 1) * width
        stacked = jnp.concatenate([y[lo:hi, :width], y[lo:hi, width:]], axis=0)
        m = lax.dot_general(sel[lo:hi], stacked, NT, preferred_element_type=F32)
        m_re = m[:, :width]
        m_im = m[:, width:]
        acc_ref[t, 0] += gr * m_re - gi * m_im
        acc_ref[t, 1] += gr * m_im + gi * m_re


def accumulate_kernel(*refs, slots, width, scale, has_prior, final, counts):
    groups = len(counts)
    g_refs = refs[:groups]
    refs = refs[groups:]
    if has_prior:
        (ti_ref, ph_ref, far_ref, slot_ref, cj_ref, prior_hbm, out_ref,
         acc_ref, sel_ref, prior_ref, sem) = refs
    else:
        ti_ref, ph_ref, far_ref, slot_ref, cj_ref, out_ref, acc_ref, sel_ref = refs
    w = pl.program_id(0)
    last = pl.num_programs(0) - 1
    nt = 2 * slots
    lanes = lax.broadcasted_iota(jnp.int32, (width, width), 1).astype(F32)

    def columns():
        far = far_ref[...]
        rows = [ti_ref[pl.ds(s, 1), :] for s in range(slots)]
        for s in range(slots):
            pick = slot_ref[s]
            rows.append(jnp.where(pick == 0, far[0:1], far[1:2]))
        rows.append(cj_ref[...])
        block = jnp.concatenate(rows, axis=0).astype(F32)
        block = jnp.concatenate([block, jnp.zeros((128 - block.shape[0], width), F32)], axis=0)
        return block.T

    @pl.when(w == 0)
    def _():
        acc_ref[...] = jnp.zeros(acc_ref.shape, F32)
        if has_prior:
            pltpu.make_async_copy(prior_hbm, prior_ref, sem).start()
        cols = columns()
        for t in range(nt):
            sel_ref[t * width:(t + 1) * width] = (cols[:, t:t + 1] == lanes).astype(BF16)

    offset = 0
    for g_ref, count in zip(g_refs, counts):
        @pl.when((w >= offset) & (w < offset + count))
        def _():
            add_walker(g_ref, sel_ref, acc_ref, slots, width)

        offset += count

    @pl.when(w == last)
    def _():
        if has_prior:
            pltpu.make_async_copy(prior_hbm, prior_ref, sem).wait()
        if not final:
            if has_prior:
                out_ref[...] = acc_ref[...] + prior_ref[...]
            else:
                out_ref[...] = acc_ref[...]
            return
        cols = columns()
        q = (cols[:, nt:nt + 1] == lanes).astype(BF16)
        far = far_ref[...]
        partner = [jnp.where(slot_ref[s] == 0, far[2:3], far[3:4]) for s in range(slots)]
        partner = jnp.concatenate(partner + [jnp.zeros((8 - slots, width), jnp.int32)], axis=0)
        partner = lax.dot_general(partner.astype(F32).astype(BF16), q, NT, preferred_element_type=F32)
        levels = jnp.concatenate([ph_ref[...].astype(F32), partner[:slots]], axis=0)
        trig = jnp.concatenate([table(levels, COSINES), table(levels, SINES)], axis=0)
        trig_cols = jnp.concatenate([trig, jnp.zeros((128 - 2 * nt, width), F32)], axis=0).T
        for s in range(slots):
            parts = []
            for t, permute in ((s, False), (s + slots, True)):
                t_re = acc_ref[t, 0] + prior_ref[t, 0] if has_prior else acc_ref[t, 0]
                t_im = acc_ref[t, 1] + prior_ref[t, 1] if has_prior else acc_ref[t, 1]
                if permute:
                    t_re = conj_permuted(q, t_re)
                    t_im = -conj_permuted(q, t_im)
                ca = trig_cols[:, t:t + 1]
                sa = trig_cols[:, nt + t:nt + t + 1]
                cb = trig[t:t + 1]
                sb = trig[nt + t:nt + t + 1]
                rot_re = ca * cb + sa * sb
                rot_im = sa * cb - ca * sb
                parts.append((rot_re * t_re - rot_im * t_im, rot_re * t_im + rot_im * t_re))
            (own_re, own_im), (mir_re, mir_im) = parts
            out_ref[s, 0] = (own_re + mir_re) * scale
            out_ref[s, 1] = (own_im + mir_im) * scale


def walker_spec(width, offset, count):
    return pl.BlockSpec((1, 2, width, width), lambda w: (jnp.clip(w - offset, 0, count - 1), 0, 0, 0))


def accumulate(walkers, info, prior, final, slots, width, scale):
    has_prior = prior is not None
    counts = tuple(g.shape[0] for g in walkers)
    kernel = functools.partial(
        accumulate_kernel, slots=slots, width=width, scale=scale, has_prior=has_prior, final=final, counts=counts
    )
    full = lambda shape: pl.BlockSpec(shape, lambda w: (0,) * len(shape))
    acc_shape = (2 * slots, 2, width, width)
    out_shape = (slots, 2, width, width) if final else acc_shape
    ti, ph, far, slot, cj = info
    offsets = [sum(counts[:k]) for k in range(len(counts))]
    in_specs = [walker_spec(width, o, c) for o, c in zip(offsets, counts)] + [
        full(ti.shape),
        full(ph.shape),
        full(far.shape),
        pl.BlockSpec(memory_space=pltpu.SMEM),
        full(cj.shape),
    ]
    scratch = [pltpu.VMEM(acc_shape, F32), pltpu.VMEM((2 * slots * width, width), BF16)]
    operands = list(walkers) + [ti, ph, far, slot, cj]
    if has_prior:
        in_specs.append(pl.BlockSpec(memory_space=pl.ANY))
        scratch += [pltpu.VMEM(acc_shape, F32), pltpu.SemaphoreType.DMA(())]
        operands.append(prior)
    steps = sum(counts)
    flops = steps * 2 * slots * 8 * width**3 + (12 * slots * 2 * width**3 if final else 0)
    moved = sum(g.size for g in walkers) * 2 + 4 * math.prod(out_shape) + (4 * math.prod(acc_shape) if has_prior else 0)
    return pl.pallas_call(
        kernel,
        grid=(steps,),
        cost_estimate=pl.CostEstimate(flops=flops, transcendentals=0, bytes_accessed=moved),
        in_specs=in_specs,
        out_specs=full(out_shape),
        out_shape=jax.ShapeDtypeStruct(out_shape, F32),
        scratch_shapes=scratch,
        compiler_params=pltpu.CompilerParams(dimension_semantics=("arbitrary",)),
    )(*operands)


def local(greens, transfer_index, phase_index, partner_slot, conj_index):
    slots = transfer_index.shape[0]
    width = greens.shape[-1]
    blocks = lax.axis_size("blk")
    halfway = lax.axis_size("xfer") // 2
    scale = 0.5 / math.sqrt(blocks)
    assert blocks % 2 == 0 and blocks & (blocks - 1) == 0 and 4 * slots + 1 <= 128

    swap = [(i, i ^ 1) for i in range(blocks)]
    sibling = lax.ppermute(greens, "blk", swap)
    fetched = [lax.ppermute(greens, "blk", [(i, i ^ (2 * m)) for i in range(blocks)]) for m in range(1, blocks // 2)]
    far = passed_along(jnp.concatenate([transfer_index, phase_index], axis=0), "xfer", halfway)
    info = (transfer_index, phase_index, far, partner_slot, conj_index.reshape(1, width))
    run = functools.partial(accumulate, info=info, slots=slots, width=width, scale=scale)

    if not fetched:
        return run([greens, sibling], prior=None, final=True)
    partial_sums = run([greens, sibling], prior=None, final=False)
    partial_sums, fetched = lax.optimization_barrier((partial_sums, fetched))
    near = jnp.concatenate(fetched, axis=0)
    forwarded = lax.ppermute(near, "blk", swap)
    partial_sums = run(fetched, prior=partial_sums, final=False)
    return run([forwarded], prior=partial_sums, final=True)


def solution(mesh):
    in_specs = (
        P("blk", None, None, None),
        P(("blk", "xfer"), None),
        P(("blk", "xfer"), None),
        P(("blk", "xfer")),
        P(),
    )
    out_specs = P(("blk", "xfer"), None, None, None)
    return jax.shard_map(local, mesh=mesh, in_specs=in_specs, out_specs=out_specs, check_vma=False)
```

```python
import functools
import math

import jax
import jax.numpy as jnp
from jax import lax
from jax.experimental import pallas as pl
from jax.experimental.pallas import tpu as pltpu
from jax.sharding import PartitionSpec as P

NPH = 8
F32 = jnp.float32
BF16 = jnp.bfloat16
NT = (((1,), (1,)), ((), ()))
CHUNK = 3
ROOT_HALF = math.sqrt(0.5)
COSINES = (1.0, ROOT_HALF, 0.0, -ROOT_HALF, -1.0, -ROOT_HALF, 0.0, ROOT_HALF)
SINES = (0.0, ROOT_HALF, 1.0, ROOT_HALF, 0.0, -ROOT_HALF, -1.0, -ROOT_HALF)


def passed_along(value, axis, by):
    size = lax.axis_size(axis)
    return lax.ppermute(value, axis, [(i, (i + by) % size) for i in range(size)])


def split3(x):
    hi = x.astype(BF16)
    r1 = x - hi.astype(F32)
    mid = r1.astype(BF16)
    lo = (r1 - mid.astype(F32)).astype(BF16)
    return (hi, mid, lo)


def conj_permuted(q, x):
    total = None
    for piece in split3(x):
        rows = jnp.dot(q, piece, preferred_element_type=F32).astype(BF16)
        moved = lax.dot_general(q, rows, NT, preferred_element_type=F32)
        total = moved if total is None else total + moved
    return total


def table(levels, values):
    out = jnp.zeros(levels.shape, F32)
    for k, v in enumerate(values):
        out = jnp.where(levels == k, v, out)
    return out


def add_walkers(blocks, sel_ref, acc_ref, slots, width):
    sel = sel_ref[...]
    terms = []
    for g_ref, k in blocks:
        g_re = g_ref[k, 0]
        g_im = g_ref[k, 1]
        y = jnp.dot(sel, jnp.concatenate([g_re, g_im], axis=1), preferred_element_type=F32).astype(BF16)
        terms.append((g_re.astype(F32), g_im.astype(F32), y))
    for t in range(2 * slots):
        lo, hi = t * width, (t + 1) * width
        acc_re = acc_ref[t, 0]
        acc_im = acc_ref[t, 1]
        for gr, gi, y in terms:
            stacked = jnp.concatenate([y[lo:hi, :width], y[lo:hi, width:]], axis=0)
            m = lax.dot_general(sel[lo:hi], stacked, NT, preferred_element_type=F32)
            m_re = m[:, :width]
            m_im = m[:, width:]
            acc_re = acc_re + (gr * m_re - gi * m_im)
            acc_im = acc_im + (gr * m_im + gi * m_re)
        acc_ref[t, 0] = acc_re
        acc_ref[t, 1] = acc_im


def accumulate_kernel(*refs, slots, width, scale, has_prior, final, counts):
    groups = len(counts)
    g_refs = refs[:groups]
    refs = refs[groups:]
    if has_prior:
        (ti_ref, ph_ref, far_ref, slot_ref, cj_ref, prior_hbm, out_ref,
         acc_ref, sel_ref, prior_ref, sem) = refs
    else:
        ti_ref, ph_ref, far_ref, slot_ref, cj_ref, out_ref, acc_ref, sel_ref = refs
    w = pl.program_id(0)
    last = pl.num_programs(0) - 1
    nt = 2 * slots
    lanes = lax.broadcasted_iota(jnp.int32, (width, width), 1).astype(F32)

    def columns():
        far = far_ref[...]
        rows = [ti_ref[pl.ds(s, 1), :] for s in range(slots)]
        for s in range(slots):
            pick = slot_ref[s]
            rows.append(jnp.where(pick == 0, far[0:1], far[1:2]))
        rows.append(cj_ref[...])
        block = jnp.concatenate(rows, axis=0).astype(F32)
        block = jnp.concatenate([block, jnp.zeros((128 - block.shape[0], width), F32)], axis=0)
        return block.T

    @pl.when(w == 0)
    def _():
        acc_ref[...] = jnp.zeros(acc_ref.shape, F32)
        if has_prior:
            pltpu.make_async_copy(prior_hbm, prior_ref, sem).start()
        cols = columns()
        for t in range(nt):
            sel_ref[t * width:(t + 1) * width] = (cols[:, t:t + 1] == lanes).astype(BF16)

    pending = [(g_ref, k) for g_ref, count in zip(g_refs, counts) for k in range(count)]
    for start in range(0, len(pending), CHUNK):
        add_walkers(pending[start:start + CHUNK], sel_ref, acc_ref, slots, width)

    @pl.when(w == last)
    def _():
        if has_prior:
            pltpu.make_async_copy(prior_hbm, prior_ref, sem).wait()
        if not final:
            if has_prior:
                out_ref[...] = acc_ref[...] + prior_ref[...]
            else:
                out_ref[...] = acc_ref[...]
            return
        cols = columns()
        q = (cols[:, nt:nt + 1] == lanes).astype(BF16)
        far = far_ref[...]
        partner = [jnp.where(slot_ref[s] == 0, far[2:3], far[3:4]) for s in range(slots)]
        partner = jnp.concatenate(partner + [jnp.zeros((8 - slots, width), jnp.int32)], axis=0)
        partner = lax.dot_general(partner.astype(F32).astype(BF16), q, NT, preferred_element_type=F32)
        levels = jnp.concatenate([ph_ref[...].astype(F32), partner[:slots]], axis=0)
        trig = jnp.concatenate([table(levels, COSINES), table(levels, SINES)], axis=0)
        trig_cols = jnp.concatenate([trig, jnp.zeros((128 - 2 * nt, width), F32)], axis=0).T
        for s in range(slots):
            parts = []
            for t, permute in ((s, False), (s + slots, True)):
                t_re = acc_ref[t, 0] + prior_ref[t, 0] if has_prior else acc_ref[t, 0]
                t_im = acc_ref[t, 1] + prior_ref[t, 1] if has_prior else acc_ref[t, 1]
                if permute:
                    t_re = conj_permuted(q, t_re)
                    t_im = -conj_permuted(q, t_im)
                ca = trig_cols[:, t:t + 1]
                sa = trig_cols[:, nt + t:nt + t + 1]
                cb = trig[t:t + 1]
                sb = trig[nt + t:nt + t + 1]
                rot_re = ca * cb + sa * sb
                rot_im = sa * cb - ca * sb
                parts.append((rot_re * t_re - rot_im * t_im, rot_re * t_im + rot_im * t_re))
            (own_re, own_im), (mir_re, mir_im) = parts
            out_ref[s, 0] = (own_re + mir_re) * scale
            out_ref[s, 1] = (own_im + mir_im) * scale


def walker_spec(width, offset, count):
    return pl.BlockSpec((1, 2, width, width), lambda w: (jnp.clip(w - offset, 0, count - 1), 0, 0, 0))


def accumulate(walkers, info, prior, final, slots, width, scale):
    has_prior = prior is not None
    counts = tuple(g.shape[0] for g in walkers)
    kernel = functools.partial(
        accumulate_kernel, slots=slots, width=width, scale=scale, has_prior=has_prior, final=final, counts=counts
    )
    full = lambda shape: pl.BlockSpec(shape, lambda w: (0,) * len(shape))
    acc_shape = (2 * slots, 2, width, width)
    out_shape = (slots, 2, width, width) if final else acc_shape
    ti, ph, far, slot, cj = info
    in_specs = [full(g.shape) for g in walkers] + [
        full(ti.shape),
        full(ph.shape),
        full(far.shape),
        pl.BlockSpec(memory_space=pltpu.SMEM),
        full(cj.shape),
    ]
    scratch = [pltpu.VMEM(acc_shape, F32), pltpu.VMEM((2 * slots * width, width), BF16)]
    operands = list(walkers) + [ti, ph, far, slot, cj]
    if has_prior:
        in_specs.append(pl.BlockSpec(memory_space=pl.ANY))
        scratch += [pltpu.VMEM(acc_shape, F32), pltpu.SemaphoreType.DMA(())]
        operands.append(prior)
    steps = sum(counts)
    flops = steps * 2 * slots * 8 * width**3 + (12 * slots * 2 * width**3 if final else 0)
    moved = sum(g.size for g in walkers) * 2 + 4 * math.prod(out_shape) + (4 * math.prod(acc_shape) if has_prior else 0)
    return pl.pallas_call(
        kernel,
        grid=(1,),
        cost_estimate=pl.CostEstimate(flops=flops, transcendentals=0, bytes_accessed=moved),
        in_specs=in_specs,
        out_specs=full(out_shape),
        out_shape=jax.ShapeDtypeStruct(out_shape, F32),
        scratch_shapes=scratch,
        compiler_params=pltpu.CompilerParams(dimension_semantics=("arbitrary",)),
    )(*operands)


def local(greens, transfer_index, phase_index, partner_slot, conj_index):
    slots = transfer_index.shape[0]
    width = greens.shape[-1]
    blocks = lax.axis_size("blk")
    halfway = lax.axis_size("xfer") // 2
    scale = 0.5 / math.sqrt(blocks)
    assert blocks % 2 == 0 and blocks & (blocks - 1) == 0 and 4 * slots + 1 <= 128

    swap = [(i, i ^ 1) for i in range(blocks)]
    sibling = lax.ppermute(greens, "blk", swap)
    fetched = [lax.ppermute(greens, "blk", [(i, i ^ (2 * m)) for i in range(blocks)]) for m in range(1, blocks // 2)]
    far = passed_along(jnp.concatenate([transfer_index, phase_index], axis=0), "xfer", halfway)
    info = (transfer_index, phase_index, far, partner_slot, conj_index.reshape(1, width))
    run = functools.partial(accumulate, info=info, slots=slots, width=width, scale=scale)

    if not fetched:
        return run([greens, sibling], prior=None, final=True)
    partial_sums = run([greens, sibling], prior=None, final=False)
    partial_sums, fetched = lax.optimization_barrier((partial_sums, fetched))
    near = jnp.concatenate(fetched, axis=0)
    forwarded = lax.ppermute(near, "blk", swap)
    partial_sums = run(fetched, prior=partial_sums, final=False)
    return run([forwarded], prior=partial_sums, final=True)


def solution(mesh):
    in_specs = (
        P("blk", None, None, None),
        P(("blk", "xfer"), None),
        P(("blk", "xfer"), None),
        P(("blk", "xfer")),
        P(),
    )
    out_specs = P(("blk", "xfer"), None, None, None)
    return jax.shard_map(local, mesh=mesh, in_specs=in_specs, out_specs=out_specs, check_vma=False)
```

```python
import functools
import math

import jax
import jax.numpy as jnp
from jax import lax
from jax.experimental import pallas as pl
from jax.experimental.pallas import tpu as pltpu
from jax.sharding import PartitionSpec as P

NPH = 8
F32 = jnp.float32
BF16 = jnp.bfloat16
NT = (((1,), (1,)), ((), ()))
CHUNK = 3
ROOT_HALF = math.sqrt(0.5)
COSINES = (1.0, ROOT_HALF, 0.0, -ROOT_HALF, -1.0, -ROOT_HALF, 0.0, ROOT_HALF)
SINES = (0.0, ROOT_HALF, 1.0, ROOT_HALF, 0.0, -ROOT_HALF, -1.0, -ROOT_HALF)


def passed_along(value, axis, by):
    size = lax.axis_size(axis)
    return lax.ppermute(value, axis, [(i, (i + by) % size) for i in range(size)])


def split2(x):
    hi = x.astype(BF16)
    return (hi, (x - hi.astype(F32)).astype(BF16))


def conj_permuted(q, x):
    total = None
    for piece in split2(x):
        rows = jnp.dot(q, piece, preferred_element_type=F32).astype(BF16)
        moved = lax.dot_general(q, rows, NT, preferred_element_type=F32)
        total = moved if total is None else total + moved
    return total


def table(levels, values):
    out = jnp.zeros(levels.shape, F32)
    for k, v in enumerate(values):
        out = jnp.where(levels == k, v, out)
    return out


def add_walkers(blocks, sel_ref, acc_ref, slots, width):
    sel = sel_ref[...]
    terms = []
    for g_ref, k in blocks:
        g_re = g_ref[k, 0]
        g_im = g_ref[k, 1]
        y = jnp.dot(sel, jnp.concatenate([g_re, g_im], axis=1), preferred_element_type=F32).astype(BF16)
        terms.append((g_re.astype(F32), g_im.astype(F32), y))
    for t in range(2 * slots):
        lo, hi = t * width, (t + 1) * width
        acc_re = acc_ref[t, 0]
        acc_im = acc_ref[t, 1]
        for gr, gi, y in terms:
            stacked = jnp.concatenate([y[lo:hi, :width], y[lo:hi, width:]], axis=0)
            m = lax.dot_general(sel[lo:hi], stacked, NT, preferred_element_type=F32)
            m_re = m[:, :width]
            m_im = m[:, width:]
            acc_re = acc_re + (gr * m_re - gi * m_im)
            acc_im = acc_im + (gr * m_im + gi * m_re)
        acc_ref[t, 0] = acc_re
        acc_ref[t, 1] = acc_im


def accumulate_kernel(*refs, slots, width, scale, has_prior, final, counts):
    groups = len(counts)
    g_refs = refs[:groups]
    refs = refs[groups:]
    if has_prior:
        (ti_ref, ph_ref, far_ref, slot_ref, cj_ref, prior_hbm, out_ref,
         acc_ref, sel_ref, prior_ref, sem) = refs
    else:
        ti_ref, ph_ref, far_ref, slot_ref, cj_ref, out_ref, acc_ref, sel_ref = refs
    w = pl.program_id(0)
    last = pl.num_programs(0) - 1
    nt = 2 * slots
    lanes = lax.broadcasted_iota(jnp.int32, (width, width), 1).astype(F32)

    def columns():
        far = far_ref[...]
        rows = [ti_ref[pl.ds(s, 1), :] for s in range(slots)]
        for s in range(slots):
            pick = slot_ref[s]
            rows.append(jnp.where(pick == 0, far[0:1], far[1:2]))
        rows.append(cj_ref[...])
        block = jnp.concatenate(rows, axis=0).astype(F32)
        block = jnp.concatenate([block, jnp.zeros((128 - block.shape[0], width), F32)], axis=0)
        return block.T

    @pl.when(w == 0)
    def _():
        acc_ref[...] = jnp.zeros(acc_ref.shape, F32)
        if has_prior:
            pltpu.make_async_copy(prior_hbm, prior_ref, sem).start()
        cols = columns()
        for t in range(nt):
            sel_ref[t * width:(t + 1) * width] = (cols[:, t:t + 1] == lanes).astype(BF16)

    pending = [(g_ref, k) for g_ref, count in zip(g_refs, counts) for k in range(count)]
    for start in range(0, len(pending), CHUNK):
        add_walkers(pending[start:start + CHUNK], sel_ref, acc_ref, slots, width)

    @pl.when(w == last)
    def _():
        if has_prior:
            pltpu.make_async_copy(prior_hbm, prior_ref, sem).wait()
        if not final:
            if has_prior:
                out_ref[...] = acc_ref[...] + prior_ref[...]
            else:
                out_ref[...] = acc_ref[...]
            return
        cols = columns()
        q = (cols[:, nt:nt + 1] == lanes).astype(BF16)
        far = far_ref[...]
        partner = [jnp.where(slot_ref[s] == 0, far[2:3], far[3:4]) for s in range(slots)]
        partner = jnp.concatenate(partner + [jnp.zeros((8 - slots, width), jnp.int32)], axis=0)
        partner = lax.dot_general(partner.astype(F32).astype(BF16), q, NT, preferred_element_type=F32)
        levels = jnp.concatenate([ph_ref[...].astype(F32), partner[:slots]], axis=0)
        trig = jnp.concatenate([table(levels, COSINES), table(levels, SINES)], axis=0)
        trig_cols = jnp.concatenate([trig, jnp.zeros((128 - 2 * nt, width), F32)], axis=0).T
        for s in range(slots):
            parts = []
            for t, permute in ((s, False), (s + slots, True)):
                t_re = acc_ref[t, 0] + prior_ref[t, 0] if has_prior else acc_ref[t, 0]
                t_im = acc_ref[t, 1] + prior_ref[t, 1] if has_prior else acc_ref[t, 1]
                if permute:
                    t_re = conj_permuted(q, t_re)
                    t_im = -conj_permuted(q, t_im)
                ca = trig_cols[:, t:t + 1]
                sa = trig_cols[:, nt + t:nt + t + 1]
                cb = trig[t:t + 1]
                sb = trig[nt + t:nt + t + 1]
                rot_re = ca * cb + sa * sb
                rot_im = sa * cb - ca * sb
                parts.append((rot_re * t_re - rot_im * t_im, rot_re * t_im + rot_im * t_re))
            (own_re, own_im), (mir_re, mir_im) = parts
            out_ref[s, 0] = (own_re + mir_re) * scale
            out_ref[s, 1] = (own_im + mir_im) * scale


def walker_spec(width, offset, count):
    return pl.BlockSpec((1, 2, width, width), lambda w: (jnp.clip(w - offset, 0, count - 1), 0, 0, 0))


def accumulate(walkers, info, prior, final, slots, width, scale):
    has_prior = prior is not None
    counts = tuple(g.shape[0] for g in walkers)
    kernel = functools.partial(
        accumulate_kernel, slots=slots, width=width, scale=scale, has_prior=has_prior, final=final, counts=counts
    )
    full = lambda shape: pl.BlockSpec(shape, lambda w: (0,) * len(shape))
    acc_shape = (2 * slots, 2, width, width)
    out_shape = (slots, 2, width, width) if final else acc_shape
    ti, ph, far, slot, cj = info
    in_specs = [full(g.shape) for g in walkers] + [
        full(ti.shape),
        full(ph.shape),
        full(far.shape),
        pl.BlockSpec(memory_space=pltpu.SMEM),
        full(cj.shape),
    ]
    scratch = [pltpu.VMEM(acc_shape, F32), pltpu.VMEM((2 * slots * width, width), BF16)]
    operands = list(walkers) + [ti, ph, far, slot, cj]
    if has_prior:
        in_specs.append(pl.BlockSpec(memory_space=pl.ANY))
        scratch += [pltpu.VMEM(acc_shape, F32), pltpu.SemaphoreType.DMA(())]
        operands.append(prior)
    steps = sum(counts)
    flops = steps * 2 * slots * 8 * width**3 + (8 * slots * 2 * width**3 if final else 0)
    moved = sum(g.size for g in walkers) * 2 + 4 * math.prod(out_shape) + (4 * math.prod(acc_shape) if has_prior else 0)
    return pl.pallas_call(
        kernel,
        grid=(1,),
        cost_estimate=pl.CostEstimate(flops=flops, transcendentals=0, bytes_accessed=moved),
        in_specs=in_specs,
        out_specs=full(out_shape),
        out_shape=jax.ShapeDtypeStruct(out_shape, F32),
        scratch_shapes=scratch,
        compiler_params=pltpu.CompilerParams(dimension_semantics=("arbitrary",)),
    )(*operands)


def local(greens, transfer_index, phase_index, partner_slot, conj_index):
    slots = transfer_index.shape[0]
    width = greens.shape[-1]
    blocks = lax.axis_size("blk")
    halfway = lax.axis_size("xfer") // 2
    scale = 0.5 / math.sqrt(blocks)
    assert blocks % 2 == 0 and blocks & (blocks - 1) == 0 and 4 * slots + 1 <= 128

    swap = [(i, i ^ 1) for i in range(blocks)]
    sibling = lax.ppermute(greens, "blk", swap)
    fetched = [lax.ppermute(greens, "blk", [(i, i ^ (2 * m)) for i in range(blocks)]) for m in range(1, blocks // 2)]
    far = passed_along(jnp.concatenate([transfer_index, phase_index], axis=0), "xfer", halfway)
    info = (transfer_index, phase_index, far, partner_slot, conj_index.reshape(1, width))
    run = functools.partial(accumulate, info=info, slots=slots, width=width, scale=scale)

    if not fetched:
        return run([greens, sibling], prior=None, final=True)
    partial_sums = run([greens, sibling], prior=None, final=False)
    partial_sums, fetched = lax.optimization_barrier((partial_sums, fetched))
    near = jnp.concatenate(fetched, axis=0)
    forwarded = lax.ppermute(near, "blk", swap)
    partial_sums = run(fetched, prior=partial_sums, final=False)
    return run([forwarded], prior=partial_sums, final=True)


def solution(mesh):
    in_specs = (
        P("blk", None, None, None),
        P(("blk", "xfer"), None),
        P(("blk", "xfer"), None),
        P(("blk", "xfer")),
        P(),
    )
    out_specs = P(("blk", "xfer"), None, None, None)
    return jax.shard_map(local, mesh=mesh, in_specs=in_specs, out_specs=out_specs, check_vma=False)
```

```python
import functools
import math

import jax
import jax.numpy as jnp
from jax import lax
from jax.experimental import pallas as pl
from jax.experimental.pallas import tpu as pltpu
from jax.sharding import PartitionSpec as P

NPH = 8
F32 = jnp.float32
BF16 = jnp.bfloat16
NT = (((1,), (1,)), ((), ()))
CHUNK = 3
ROOT_HALF = math.sqrt(0.5)
COSINES = (1.0, ROOT_HALF, 0.0, -ROOT_HALF, -1.0, -ROOT_HALF, 0.0, ROOT_HALF)
SINES = (0.0, ROOT_HALF, 1.0, ROOT_HALF, 0.0, -ROOT_HALF, -1.0, -ROOT_HALF)


def passed_along(value, axis, by):
    size = lax.axis_size(axis)
    return lax.ppermute(value, axis, [(i, (i + by) % size) for i in range(size)])


def split2(x):
    hi = x.astype(BF16)
    return (hi, (x - hi.astype(F32)).astype(BF16))


def conj_permuted(q, x):
    total = None
    for piece in split2(x):
        rows = jnp.dot(q, piece, preferred_element_type=F32).astype(BF16)
        moved = lax.dot_general(q, rows, NT, preferred_element_type=F32)
        total = moved if total is None else total + moved
    return total


def table(levels, values):
    out = jnp.zeros(levels.shape, F32)
    for k, v in enumerate(values):
        out = jnp.where(levels == k, v, out)
    return out


def add_walkers(blocks, sel_ref, acc_ref, slots, width):
    sel = sel_ref[...]
    terms = []
    for g_ref, k in blocks:
        g_re = g_ref[k, 0]
        g_im = g_ref[k, 1]
        y = jnp.dot(sel, jnp.concatenate([g_re, g_im], axis=1), preferred_element_type=F32).astype(BF16)
        terms.append((g_re.astype(F32), g_im.astype(F32), y))
    for t in range(2 * slots):
        lo, hi = t * width, (t + 1) * width
        acc_re = acc_ref[t, 0]
        acc_im = acc_ref[t, 1]
        for gr, gi, y in terms:
            stacked = jnp.concatenate([y[lo:hi, :width], y[lo:hi, width:]], axis=0)
            m = lax.dot_general(sel[lo:hi], stacked, NT, preferred_element_type=F32)
            m_re = m[:, :width]
            m_im = m[:, width:]
            acc_re = acc_re + (gr * m_re - gi * m_im)
            acc_im = acc_im + (gr * m_im + gi * m_re)
        acc_ref[t, 0] = acc_re
        acc_ref[t, 1] = acc_im


def accumulate_kernel(*refs, slots, width, scale, has_prior, final, counts):
    groups = len(counts)
    g_refs = refs[:groups]
    refs = refs[groups:]
    if has_prior:
        (ti_ref, ph_ref, far_ref, slot_ref, cj_ref, prior_hbm, out_ref,
         acc_ref, sel_ref, prior_ref, sem) = refs
    else:
        ti_ref, ph_ref, far_ref, slot_ref, cj_ref, out_ref, acc_ref, sel_ref = refs
    w = pl.program_id(0)
    last = pl.num_programs(0) - 1
    nt = 2 * slots
    lanes = lax.broadcasted_iota(jnp.int32, (width, width), 1).astype(F32)

    def columns():
        far = far_ref[...]
        rows = [ti_ref[pl.ds(s, 1), :] for s in range(slots)]
        for s in range(slots):
            pick = slot_ref[s]
            rows.append(jnp.where(pick == 0, far[0:1], far[1:2]))
        rows.append(cj_ref[...])
        block = jnp.concatenate(rows, axis=0).astype(F32)
        block = jnp.concatenate([block, jnp.zeros((128 - block.shape[0], width), F32)], axis=0)
        return block.T

    @pl.when(w == 0)
    def _():
        acc_ref[...] = jnp.zeros(acc_ref.shape, F32)
        if has_prior:
            pltpu.make_async_copy(prior_hbm, prior_ref, sem).start()
        cols = columns()
        for t in range(nt):
            sel_ref[t * width:(t + 1) * width] = (cols[:, t:t + 1] == lanes).astype(BF16)

    pending = [(g_ref, k) for g_ref, count in zip(g_refs, counts) for k in range(count)]
    for start in range(0, len(pending), CHUNK):
        add_walkers(pending[start:start + CHUNK], sel_ref, acc_ref, slots, width)

    @pl.when(w == last)
    def _():
        if has_prior:
            pltpu.make_async_copy(prior_hbm, prior_ref, sem).wait()
        if not final:
            if has_prior:
                out_ref[...] = acc_ref[...] + prior_ref[...]
            else:
                out_ref[...] = acc_ref[...]
            return
        cols = columns()
        q = (cols[:, nt:nt + 1] == lanes).astype(BF16)
        far = far_ref[...]
        partner = [jnp.where(slot_ref[s] == 0, far[2:3], far[3:4]) for s in range(slots)]
        partner = jnp.concatenate(partner + [jnp.zeros((8 - slots, width), jnp.int32)], axis=0)
        partner = lax.dot_general(partner.astype(F32).astype(BF16), q, NT, preferred_element_type=F32)
        levels = jnp.concatenate([ph_ref[...].astype(F32), partner[:slots]], axis=0)
        trig = jnp.concatenate([table(levels, COSINES), table(levels, SINES)], axis=0)
        trig_cols = jnp.concatenate([trig, jnp.zeros((128 - 2 * nt, width), F32)], axis=0).T
        for s in range(slots):
            parts = []
            for t, permute in ((s, False), (s + slots, True)):
                t_re = acc_ref[t, 0] + prior_ref[t, 0] if has_prior else acc_ref[t, 0]
                t_im = acc_ref[t, 1] + prior_ref[t, 1] if has_prior else acc_ref[t, 1]
                if permute:
                    t_re = conj_permuted(q, t_re)
                    t_im = -conj_permuted(q, t_im)
                ca = trig_cols[:, t:t + 1]
                sa = trig_cols[:, nt + t:nt + t + 1]
                cb = trig[t:t + 1]
                sb = trig[nt + t:nt + t + 1]
                rot_re = ca * cb + sa * sb
                rot_im = sa * cb - ca * sb
                parts.append((rot_re * t_re - rot_im * t_im, rot_re * t_im + rot_im * t_re))
            (own_re, own_im), (mir_re, mir_im) = parts
            out_ref[s, 0] = (own_re + mir_re) * scale
            out_ref[s, 1] = (own_im + mir_im) * scale


def walker_spec(width, offset, count):
    return pl.BlockSpec((1, 2, width, width), lambda w: (jnp.clip(w - offset, 0, count - 1), 0, 0, 0))


def accumulate(walkers, info, prior, final, slots, width, scale):
    has_prior = prior is not None
    counts = tuple(g.shape[0] for g in walkers)
    kernel = functools.partial(
        accumulate_kernel, slots=slots, width=width, scale=scale, has_prior=has_prior, final=final, counts=counts
    )
    full = lambda shape: pl.BlockSpec(shape, lambda w: (0,) * len(shape))
    acc_shape = (2 * slots, 2, width, width)
    out_shape = (slots, 2, width, width) if final else acc_shape
    ti, ph, far, slot, cj = info
    in_specs = [full(g.shape) for g in walkers] + [
        full(ti.shape),
        full(ph.shape),
        full(far.shape),
        pl.BlockSpec(memory_space=pltpu.SMEM),
        full(cj.shape),
    ]
    scratch = [pltpu.VMEM(acc_shape, F32), pltpu.VMEM((2 * slots * width, width), BF16)]
    operands = list(walkers) + [ti, ph, far, slot, cj]
    if has_prior:
        in_specs.append(pl.BlockSpec(memory_space=pl.ANY))
        scratch += [pltpu.VMEM(acc_shape, F32), pltpu.SemaphoreType.DMA(())]
        operands.append(prior)
    steps = sum(counts)
    flops = steps * 2 * slots * 8 * width**3 + (8 * slots * 2 * width**3 if final else 0)
    moved = sum(g.size for g in walkers) * 2 + 4 * math.prod(out_shape) + (4 * math.prod(acc_shape) if has_prior else 0)
    return pl.pallas_call(
        kernel,
        grid=(1,),
        cost_estimate=pl.CostEstimate(flops=flops, transcendentals=0, bytes_accessed=moved),
        in_specs=in_specs,
        out_specs=full(out_shape),
        out_shape=jax.ShapeDtypeStruct(out_shape, F32),
        scratch_shapes=scratch,
        compiler_params=pltpu.CompilerParams(dimension_semantics=("arbitrary",)),
    )(*operands)


def local(greens, transfer_index, phase_index, partner_slot, conj_index):
    slots = transfer_index.shape[0]
    width = greens.shape[-1]
    blocks = lax.axis_size("blk")
    halfway = lax.axis_size("xfer") // 2
    scale = 0.5 / math.sqrt(blocks)
    assert blocks % 2 == 0 and blocks & (blocks - 1) == 0 and 4 * slots + 1 <= 128

    swap = [(i, i ^ 1) for i in range(blocks)]
    sibling = lax.ppermute(greens, "blk", swap)
    pair = [(j, j ^ 1) for j in range(lax.axis_size("xfer"))]
    parity = lax.axis_index("xfer") % 2
    direct, halves = [], []
    for m in range(1, blocks // 2):
        moves = [(i, i ^ (2 * m)) for i in range(blocks)]
        if bin(m).count("1") == 1 or len(pair) % 2:
            direct.append(lax.ppermute(greens, "blk", moves))
        else:
            halves.append(lax.ppermute(lax.dynamic_slice_in_dim(greens, parity, 1, axis=1), "blk", moves))
    far = passed_along(jnp.concatenate([transfer_index, phase_index], axis=0), "xfer", halfway)
    info = (transfer_index, phase_index, far, partner_slot, conj_index.reshape(1, width))
    run = functools.partial(accumulate, info=info, slots=slots, width=width, scale=scale)

    if not direct:
        return run([greens, sibling], prior=None, final=True)
    partial_sums = run([greens, sibling], prior=None, final=False)
    partial_sums, direct, halves = lax.optimization_barrier((partial_sums, direct, halves))
    theirs = [lax.ppermute(mine, "xfer", pair) for mine in halves]
    forwarded = [lax.ppermute(jnp.concatenate(direct, axis=0), "blk", swap)]
    partial_sums = run(direct, prior=partial_sums, final=False)
    if halves:
        partial_sums, theirs = lax.optimization_barrier((partial_sums, theirs))
        late = []
        for mine, other in zip(halves, theirs):
            first = jnp.where(parity == 0, mine, other)
            second = jnp.where(parity == 0, other, mine)
            late.append(jnp.concatenate([first, second], axis=1))
        late = jnp.concatenate(late, axis=0)
        forwarded += [late, lax.ppermute(late, "blk", swap)]
    return run(forwarded, prior=partial_sums, final=True)


def solution(mesh):
    in_specs = (
        P("blk", None, None, None),
        P(("blk", "xfer"), None),
        P(("blk", "xfer"), None),
        P(("blk", "xfer")),
        P(),
    )
    out_specs = P(("blk", "xfer"), None, None, None)
    return jax.shard_map(local, mesh=mesh, in_specs=in_specs, out_specs=out_specs, check_vma=False)
```

```python
import functools
import math

import jax
import jax.numpy as jnp
from jax import lax
from jax.experimental import pallas as pl
from jax.experimental.pallas import tpu as pltpu
from jax.sharding import PartitionSpec as P

NPH = 8
F32 = jnp.float32
BF16 = jnp.bfloat16
NT = (((1,), (1,)), ((), ()))
CHUNK = 3
ROOT_HALF = math.sqrt(0.5)
COSINES = (1.0, ROOT_HALF, 0.0, -ROOT_HALF, -1.0, -ROOT_HALF, 0.0, ROOT_HALF)
SINES = (0.0, ROOT_HALF, 1.0, ROOT_HALF, 0.0, -ROOT_HALF, -1.0, -ROOT_HALF)


def passed_along(value, axis, by):
    size = lax.axis_size(axis)
    return lax.ppermute(value, axis, [(i, (i + by) % size) for i in range(size)])


def split2(x):
    hi = x.astype(BF16)
    return (hi, (x - hi.astype(F32)).astype(BF16))


def conj_permuted(q, x):
    total = None
    for piece in split2(x):
        rows = jnp.dot(q, piece, preferred_element_type=F32).astype(BF16)
        moved = lax.dot_general(q, rows, NT, preferred_element_type=F32)
        total = moved if total is None else total + moved
    return total


def table(levels, values):
    out = jnp.zeros(levels.shape, F32)
    for k, v in enumerate(values):
        out = jnp.where(levels == k, v, out)
    return out


def add_walkers(blocks, sel_ref, acc_ref, slots, width):
    sel = sel_ref[...]
    terms = []
    for g_ref, k in blocks:
        g_re = g_ref[k, 0]
        g_im = g_ref[k, 1]
        y = jnp.dot(sel, jnp.concatenate([g_re, g_im], axis=1), preferred_element_type=F32).astype(BF16)
        terms.append((g_re.astype(F32), g_im.astype(F32), y))
    for t in range(2 * slots):
        lo, hi = t * width, (t + 1) * width
        acc_re = acc_ref[t, 0]
        acc_im = acc_ref[t, 1]
        for gr, gi, y in terms:
            stacked = jnp.concatenate([y[lo:hi, :width], y[lo:hi, width:]], axis=0)
            m = lax.dot_general(sel[lo:hi], stacked, NT, preferred_element_type=F32)
            m_re = m[:, :width]
            m_im = m[:, width:]
            acc_re = acc_re + (gr * m_re - gi * m_im)
            acc_im = acc_im + (gr * m_im + gi * m_re)
        acc_ref[t, 0] = acc_re
        acc_ref[t, 1] = acc_im


def accumulate_kernel(*refs, slots, width, scale, has_prior, final, counts):
    groups = len(counts)
    g_refs = refs[:groups]
    refs = refs[groups:]
    if has_prior:
        (ti_ref, ph_ref, far_ref, slot_ref, cj_ref, prior_hbm, out_ref,
         acc_ref, sel_ref, prior_ref, sem) = refs
    else:
        ti_ref, ph_ref, far_ref, slot_ref, cj_ref, out_ref, acc_ref, sel_ref = refs
    w = pl.program_id(0)
    last = pl.num_programs(0) - 1
    nt = 2 * slots
    lanes = lax.broadcasted_iota(jnp.int32, (width, width), 1).astype(F32)

    def columns():
        far = far_ref[...]
        rows = [ti_ref[pl.ds(s, 1), :] for s in range(slots)]
        for s in range(slots):
            pick = slot_ref[s]
            rows.append(jnp.where(pick == 0, far[0:1], far[1:2]))
        rows.append(cj_ref[...])
        block = jnp.concatenate(rows, axis=0).astype(F32)
        block = jnp.concatenate([block, jnp.zeros((128 - block.shape[0], width), F32)], axis=0)
        return block.T

    @pl.when(w == 0)
    def _():
        acc_ref[...] = jnp.zeros(acc_ref.shape, F32)
        if has_prior:
            pltpu.make_async_copy(prior_hbm, prior_ref, sem).start()
        cols = columns()
        for t in range(nt):
            sel_ref[t * width:(t + 1) * width] = (cols[:, t:t + 1] == lanes).astype(BF16)

    pending = [(g_ref, k) for g_ref, count in zip(g_refs, counts) for k in range(count)]
    for start in range(0, len(pending), CHUNK):
        add_walkers(pending[start:start + CHUNK], sel_ref, acc_ref, slots, width)

    @pl.when(w == last)
    def _():
        if has_prior:
            pltpu.make_async_copy(prior_hbm, prior_ref, sem).wait()
        if not final:
            if has_prior:
                out_ref[...] = acc_ref[...] + prior_ref[...]
            else:
                out_ref[...] = acc_ref[...]
            return
        cols = columns()
        q = (cols[:, nt:nt + 1] == lanes).astype(BF16)
        far = far_ref[...]
        partner = [jnp.where(slot_ref[s] == 0, far[2:3], far[3:4]) for s in range(slots)]
        partner = jnp.concatenate(partner + [jnp.zeros((8 - slots, width), jnp.int32)], axis=0)
        partner = lax.dot_general(partner.astype(F32).astype(BF16), q, NT, preferred_element_type=F32)
        levels = jnp.concatenate([ph_ref[...].astype(F32), partner[:slots]], axis=0)
        trig = jnp.concatenate([table(levels, COSINES), table(levels, SINES)], axis=0)
        trig_cols = jnp.concatenate([trig, jnp.zeros((128 - 2 * nt, width), F32)], axis=0).T
        for s in range(slots):
            parts = []
            for t, permute in ((s, False), (s + slots, True)):
                t_re = acc_ref[t, 0] + prior_ref[t, 0] if has_prior else acc_ref[t, 0]
                t_im = acc_ref[t, 1] + prior_ref[t, 1] if has_prior else acc_ref[t, 1]
                if permute:
                    t_re = conj_permuted(q, t_re)
                    t_im = -conj_permuted(q, t_im)
                ca = trig_cols[:, t:t + 1]
                sa = trig_cols[:, nt + t:nt + t + 1]
                cb = trig[t:t + 1]
                sb = trig[nt + t:nt + t + 1]
                rot_re = ca * cb + sa * sb
                rot_im = sa * cb - ca * sb
                parts.append((rot_re * t_re - rot_im * t_im, rot_re * t_im + rot_im * t_re))
            (own_re, own_im), (mir_re, mir_im) = parts
            out_ref[s, 0] = (own_re + mir_re) * scale
            out_ref[s, 1] = (own_im + mir_im) * scale


def walker_spec(width, offset, count):
    return pl.BlockSpec((1, 2, width, width), lambda w: (jnp.clip(w - offset, 0, count - 1), 0, 0, 0))


def accumulate(walkers, info, prior, final, slots, width, scale):
    has_prior = prior is not None
    counts = tuple(g.shape[0] for g in walkers)
    kernel = functools.partial(
        accumulate_kernel, slots=slots, width=width, scale=scale, has_prior=has_prior, final=final, counts=counts
    )
    full = lambda shape: pl.BlockSpec(shape, lambda w: (0,) * len(shape))
    acc_shape = (2 * slots, 2, width, width)
    out_shape = (slots, 2, width, width) if final else acc_shape
    ti, ph, far, slot, cj = info
    in_specs = [full(g.shape) for g in walkers] + [
        full(ti.shape),
        full(ph.shape),
        full(far.shape),
        pl.BlockSpec(memory_space=pltpu.SMEM),
        full(cj.shape),
    ]
    scratch = [pltpu.VMEM(acc_shape, F32), pltpu.VMEM((2 * slots * width, width), BF16)]
    operands = list(walkers) + [ti, ph, far, slot, cj]
    if has_prior:
        in_specs.append(pl.BlockSpec(memory_space=pl.ANY))
        scratch += [pltpu.VMEM(acc_shape, F32), pltpu.SemaphoreType.DMA(())]
        operands.append(prior)
    steps = sum(counts)
    flops = steps * 2 * slots * 8 * width**3 + (8 * slots * 2 * width**3 if final else 0)
    moved = sum(g.size for g in walkers) * 2 + 4 * math.prod(out_shape) + (4 * math.prod(acc_shape) if has_prior else 0)
    return pl.pallas_call(
        kernel,
        grid=(1,),
        cost_estimate=pl.CostEstimate(flops=flops, transcendentals=0, bytes_accessed=moved),
        in_specs=in_specs,
        out_specs=full(out_shape),
        out_shape=jax.ShapeDtypeStruct(out_shape, F32),
        scratch_shapes=scratch,
        compiler_params=pltpu.CompilerParams(dimension_semantics=("arbitrary",)),
    )(*operands)


def local(greens, transfer_index, phase_index, partner_slot, conj_index):
    slots = transfer_index.shape[0]
    width = greens.shape[-1]
    blocks = lax.axis_size("blk")
    halfway = lax.axis_size("xfer") // 2
    scale = 0.5 / math.sqrt(blocks)
    assert blocks % 2 == 0 and blocks & (blocks - 1) == 0 and 4 * slots + 1 <= 128

    swap = [(i, i ^ 1) for i in range(blocks)]
    sibling = lax.ppermute(greens, "blk", swap)
    fetched = [lax.ppermute(greens, "blk", [(i, i ^ (2 * m)) for i in range(blocks)]) for m in range(1, blocks // 2)]
    far = passed_along(jnp.concatenate([transfer_index, phase_index], axis=0), "xfer", halfway)
    info = (transfer_index, phase_index, far, partner_slot, conj_index.reshape(1, width))
    run = functools.partial(accumulate, info=info, slots=slots, width=width, scale=scale)

    if not fetched:
        return run([greens, sibling], prior=None, final=True)
    partial_sums = run([greens, sibling], prior=None, final=False)
    partial_sums, fetched = lax.optimization_barrier((partial_sums, [fetched[1], fetched[0]] + fetched[2:]))
    near = jnp.concatenate(fetched, axis=0)
    forwarded = lax.ppermute(near, "blk", swap)
    partial_sums = run(fetched, prior=partial_sums, final=False)
    return run([forwarded], prior=partial_sums, final=True)


def solution(mesh):
    in_specs = (
        P("blk", None, None, None),
        P(("blk", "xfer"), None),
        P(("blk", "xfer"), None),
        P(("blk", "xfer")),
        P(),
    )
    out_specs = P(("blk", "xfer"), None, None, None)
    return jax.shard_map(local, mesh=mesh, in_specs=in_specs, out_specs=out_specs, check_vma=False)
```

```python
import functools
import math

import jax
import jax.numpy as jnp
from jax import lax
from jax.experimental import pallas as pl
from jax.experimental.pallas import tpu as pltpu
from jax.sharding import PartitionSpec as P

NPH = 8
F32 = jnp.float32
BF16 = jnp.bfloat16
NT = (((1,), (1,)), ((), ()))
CHUNK = 3
ROOT_HALF = math.sqrt(0.5)
COSINES = (1.0, ROOT_HALF, 0.0, -ROOT_HALF, -1.0, -ROOT_HALF, 0.0, ROOT_HALF)
SINES = (0.0, ROOT_HALF, 1.0, ROOT_HALF, 0.0, -ROOT_HALF, -1.0, -ROOT_HALF)


def passed_along(value, axis, by):
    size = lax.axis_size(axis)
    return lax.ppermute(value, axis, [(i, (i + by) % size) for i in range(size)])


def split2(x):
    hi = x.astype(BF16)
    return (hi, (x - hi.astype(F32)).astype(BF16))


def conj_permuted(q, x):
    total = None
    for piece in split2(x):
        rows = jnp.dot(q, piece, preferred_element_type=F32).astype(BF16)
        moved = lax.dot_general(q, rows, NT, preferred_element_type=F32)
        total = moved if total is None else total + moved
    return total


def table(levels, values):
    out = jnp.zeros(levels.shape, F32)
    for k, v in enumerate(values):
        out = jnp.where(levels == k, v, out)
    return out


def add_walkers(blocks, sel_ref, acc_ref, slots, width):
    sel = sel_ref[...]
    terms = []
    for g_ref, k, copy in blocks:
        copy.wait()
        g_re = g_ref[k, 0]
        g_im = g_ref[k, 1]
        y = jnp.dot(sel, jnp.concatenate([g_re, g_im], axis=1), preferred_element_type=F32).astype(BF16)
        terms.append((g_re.astype(F32), g_im.astype(F32), y))
    for t in range(2 * slots):
        lo, hi = t * width, (t + 1) * width
        acc_re = acc_ref[t, 0]
        acc_im = acc_ref[t, 1]
        for gr, gi, y in terms:
            stacked = jnp.concatenate([y[lo:hi, :width], y[lo:hi, width:]], axis=0)
            m = lax.dot_general(sel[lo:hi], stacked, NT, preferred_element_type=F32)
            m_re = m[:, :width]
            m_im = m[:, width:]
            acc_re = acc_re + (gr * m_re - gi * m_im)
            acc_im = acc_im + (gr * m_im + gi * m_re)
        acc_ref[t, 0] = acc_re
        acc_ref[t, 1] = acc_im


def accumulate_kernel(*refs, slots, width, scale, has_prior, final, counts):
    groups = len(counts)
    g_refs = refs[:groups]
    refs = refs[groups:]
    refs, (g_buf, g_sem) = refs[:-2], refs[-2:]
    if has_prior:
        (ti_ref, ph_ref, far_ref, slot_ref, cj_ref, prior_hbm, out_ref,
         acc_ref, sel_ref, prior_ref, sem) = refs
    else:
        ti_ref, ph_ref, far_ref, slot_ref, cj_ref, out_ref, acc_ref, sel_ref = refs
    places = [(g_ref, k) for g_ref, count in zip(g_refs, counts) for k in range(count)]
    copies = [
        pltpu.make_async_copy(g_ref.at[k], g_buf.at[n], g_sem.at[n]) for n, (g_ref, k) in enumerate(places)
    ]
    w = pl.program_id(0)
    last = pl.num_programs(0) - 1
    nt = 2 * slots
    lanes = lax.broadcasted_iota(jnp.int32, (width, width), 1).astype(F32)

    def columns():
        far = far_ref[...]
        rows = [ti_ref[pl.ds(s, 1), :] for s in range(slots)]
        for s in range(slots):
            pick = slot_ref[s]
            rows.append(jnp.where(pick == 0, far[0:1], far[1:2]))
        rows.append(cj_ref[...])
        block = jnp.concatenate(rows, axis=0).astype(F32)
        block = jnp.concatenate([block, jnp.zeros((128 - block.shape[0], width), F32)], axis=0)
        return block.T

    @pl.when(w == 0)
    def _():
        for copy in copies:
            copy.start()
        acc_ref[...] = jnp.zeros(acc_ref.shape, F32)
        if has_prior:
            pltpu.make_async_copy(prior_hbm, prior_ref, sem).start()
        cols = columns()
        for t in range(nt):
            sel_ref[t * width:(t + 1) * width] = (cols[:, t:t + 1] == lanes).astype(BF16)

    pending = [(g_buf, n, copy) for n, copy in enumerate(copies)]
    for start in range(0, len(pending), CHUNK):
        add_walkers(pending[start:start + CHUNK], sel_ref, acc_ref, slots, width)

    @pl.when(w == last)
    def _():
        if has_prior:
            pltpu.make_async_copy(prior_hbm, prior_ref, sem).wait()
        if not final:
            if has_prior:
                out_ref[...] = acc_ref[...] + prior_ref[...]
            else:
                out_ref[...] = acc_ref[...]
            return
        cols = columns()
        q = (cols[:, nt:nt + 1] == lanes).astype(BF16)
        far = far_ref[...]
        partner = [jnp.where(slot_ref[s] == 0, far[2:3], far[3:4]) for s in range(slots)]
        partner = jnp.concatenate(partner + [jnp.zeros((8 - slots, width), jnp.int32)], axis=0)
        partner = lax.dot_general(partner.astype(F32).astype(BF16), q, NT, preferred_element_type=F32)
        levels = jnp.concatenate([ph_ref[...].astype(F32), partner[:slots]], axis=0)
        trig = jnp.concatenate([table(levels, COSINES), table(levels, SINES)], axis=0)
        trig_cols = jnp.concatenate([trig, jnp.zeros((128 - 2 * nt, width), F32)], axis=0).T
        for s in range(slots):
            parts = []
            for t, permute in ((s, False), (s + slots, True)):
                t_re = acc_ref[t, 0] + prior_ref[t, 0] if has_prior else acc_ref[t, 0]
                t_im = acc_ref[t, 1] + prior_ref[t, 1] if has_prior else acc_ref[t, 1]
                if permute:
                    t_re = conj_permuted(q, t_re)
                    t_im = -conj_permuted(q, t_im)
                ca = trig_cols[:, t:t + 1]
                sa = trig_cols[:, nt + t:nt + t + 1]
                cb = trig[t:t + 1]
                sb = trig[nt + t:nt + t + 1]
                rot_re = ca * cb + sa * sb
                rot_im = sa * cb - ca * sb
                parts.append((rot_re * t_re - rot_im * t_im, rot_re * t_im + rot_im * t_re))
            (own_re, own_im), (mir_re, mir_im) = parts
            out_ref[s, 0] = (own_re + mir_re) * scale
            out_ref[s, 1] = (own_im + mir_im) * scale


def walker_spec(width, offset, count):
    return pl.BlockSpec((1, 2, width, width), lambda w: (jnp.clip(w - offset, 0, count - 1), 0, 0, 0))


def accumulate(walkers, info, prior, final, slots, width, scale):
    has_prior = prior is not None
    counts = tuple(g.shape[0] for g in walkers)
    kernel = functools.partial(
        accumulate_kernel, slots=slots, width=width, scale=scale, has_prior=has_prior, final=final, counts=counts
    )
    full = lambda shape: pl.BlockSpec(shape, lambda w: (0,) * len(shape))
    acc_shape = (2 * slots, 2, width, width)
    out_shape = (slots, 2, width, width) if final else acc_shape
    ti, ph, far, slot, cj = info
    in_specs = [pl.BlockSpec(memory_space=pl.ANY) for g in walkers] + [
        full(ti.shape),
        full(ph.shape),
        full(far.shape),
        pl.BlockSpec(memory_space=pltpu.SMEM),
        full(cj.shape),
    ]
    scratch = [pltpu.VMEM(acc_shape, F32), pltpu.VMEM((2 * slots * width, width), BF16)]
    operands = list(walkers) + [ti, ph, far, slot, cj]
    tail = [pltpu.VMEM((sum(counts), 2, width, width), BF16), pltpu.SemaphoreType.DMA((sum(counts),))]
    if has_prior:
        in_specs.append(pl.BlockSpec(memory_space=pl.ANY))
        scratch += [pltpu.VMEM(acc_shape, F32), pltpu.SemaphoreType.DMA(())]
        operands.append(prior)
    steps = sum(counts)
    flops = steps * 2 * slots * 8 * width**3 + (8 * slots * 2 * width**3 if final else 0)
    moved = sum(g.size for g in walkers) * 2 + 4 * math.prod(out_shape) + (4 * math.prod(acc_shape) if has_prior else 0)
    return pl.pallas_call(
        kernel,
        grid=(1,),
        cost_estimate=pl.CostEstimate(flops=flops, transcendentals=0, bytes_accessed=moved),
        in_specs=in_specs,
        out_specs=full(out_shape),
        out_shape=jax.ShapeDtypeStruct(out_shape, F32),
        scratch_shapes=scratch + tail,
        compiler_params=pltpu.CompilerParams(dimension_semantics=("arbitrary",)),
    )(*operands)


def local(greens, transfer_index, phase_index, partner_slot, conj_index):
    slots = transfer_index.shape[0]
    width = greens.shape[-1]
    blocks = lax.axis_size("blk")
    halfway = lax.axis_size("xfer") // 2
    scale = 0.5 / math.sqrt(blocks)
    assert blocks % 2 == 0 and blocks & (blocks - 1) == 0 and 4 * slots + 1 <= 128

    swap = [(i, i ^ 1) for i in range(blocks)]
    sibling = lax.ppermute(greens, "blk", swap)
    fetched = [lax.ppermute(greens, "blk", [(i, i ^ (2 * m)) for i in range(blocks)]) for m in range(1, blocks // 2)]
    far = passed_along(jnp.concatenate([transfer_index, phase_index], axis=0), "xfer", halfway)
    info = (transfer_index, phase_index, far, partner_slot, conj_index.reshape(1, width))
    run = functools.partial(accumulate, info=info, slots=slots, width=width, scale=scale)

    if not fetched:
        return run([greens, sibling], prior=None, final=True)
    partial_sums = run([greens, sibling], prior=None, final=False)
    partial_sums, fetched = lax.optimization_barrier((partial_sums, [fetched[1], fetched[0]] + fetched[2:]))
    near = jnp.concatenate(fetched, axis=0)
    forwarded = lax.ppermute(near, "blk", swap)
    partial_sums = run(fetched, prior=partial_sums, final=False)
    return run([forwarded], prior=partial_sums, final=True)


def solution(mesh):
    in_specs = (
        P("blk", None, None, None),
        P(("blk", "xfer"), None),
        P(("blk", "xfer"), None),
        P(("blk", "xfer")),
        P(),
    )
    out_specs = P(("blk", "xfer"), None, None, None)
    return jax.shard_map(local, mesh=mesh, in_specs=in_specs, out_specs=out_specs, check_vma=False)
```

```python
import functools
import math

import jax
import jax.numpy as jnp
from jax import lax
from jax.experimental import pallas as pl
from jax.experimental.pallas import tpu as pltpu
from jax.sharding import PartitionSpec as P

NPH = 8
F32 = jnp.float32
BF16 = jnp.bfloat16
NT = (((1,), (1,)), ((), ()))
CHUNK = 3
ROOT_HALF = math.sqrt(0.5)
COSINES = (1.0, ROOT_HALF, 0.0, -ROOT_HALF, -1.0, -ROOT_HALF, 0.0, ROOT_HALF)
SINES = (0.0, ROOT_HALF, 1.0, ROOT_HALF, 0.0, -ROOT_HALF, -1.0, -ROOT_HALF)


def passed_along(value, axis, by):
    size = lax.axis_size(axis)
    return lax.ppermute(value, axis, [(i, (i + by) % size) for i in range(size)])


def split2(x):
    hi = x.astype(BF16)
    return (hi, (x - hi.astype(F32)).astype(BF16))


def conj_permuted(q, x):
    total = None
    for piece in split2(x):
        rows = jnp.dot(q, piece, preferred_element_type=F32).astype(BF16)
        moved = lax.dot_general(q, rows, NT, preferred_element_type=F32)
        total = moved if total is None else total + moved
    return total


def table(levels, values):
    out = jnp.zeros(levels.shape, F32)
    for k, v in enumerate(values):
        out = jnp.where(levels == k, v, out)
    return out


def add_walkers(blocks, sel_ref, acc_ref, slots, width, finish=None):
    sel = sel_ref[...]
    terms = []
    for g_ref, k in blocks:
        g_re = g_ref[k, 0]
        g_im = g_ref[k, 1]
        y = jnp.dot(sel, jnp.concatenate([g_re, g_im], axis=1), preferred_element_type=F32).astype(BF16)
        terms.append((g_re.astype(F32), g_im.astype(F32), y))
    for t in range(2 * slots):
        lo, hi = t * width, (t + 1) * width
        acc_re = acc_ref[t, 0]
        acc_im = acc_ref[t, 1]
        for gr, gi, y in terms:
            stacked = jnp.concatenate([y[lo:hi, :width], y[lo:hi, width:]], axis=0)
            m = lax.dot_general(sel[lo:hi], stacked, NT, preferred_element_type=F32)
            m_re = m[:, :width]
            m_im = m[:, width:]
            acc_re = acc_re + (gr * m_re - gi * m_im)
            acc_im = acc_im + (gr * m_im + gi * m_re)
        if finish is None:
            acc_ref[t, 0] = acc_re
            acc_ref[t, 1] = acc_im
        else:
            finish(t, acc_re, acc_im)


def accumulate_kernel(*refs, slots, width, scale, has_prior, final, counts):
    groups = len(counts)
    g_refs = refs[:groups]
    refs = refs[groups:]
    if not final:
        refs, out_sem = refs[:-1], refs[-1]
    if has_prior:
        (ti_ref, ph_ref, far_ref, slot_ref, cj_ref, prior_hbm, out_ref,
         acc_ref, sel_ref, prior_ref, sem) = refs
    else:
        ti_ref, ph_ref, far_ref, slot_ref, cj_ref, out_ref, acc_ref, sel_ref = refs
    w = pl.program_id(0)
    last = pl.num_programs(0) - 1
    nt = 2 * slots
    lanes = lax.broadcasted_iota(jnp.int32, (width, width), 1).astype(F32)

    def columns():
        far = far_ref[...]
        rows = [ti_ref[pl.ds(s, 1), :] for s in range(slots)]
        for s in range(slots):
            pick = slot_ref[s]
            rows.append(jnp.where(pick == 0, far[0:1], far[1:2]))
        rows.append(cj_ref[...])
        block = jnp.concatenate(rows, axis=0).astype(F32)
        block = jnp.concatenate([block, jnp.zeros((128 - block.shape[0], width), F32)], axis=0)
        return block.T

    @pl.when(w == 0)
    def _():
        acc_ref[...] = jnp.zeros(acc_ref.shape, F32)
        if has_prior:
            pltpu.make_async_copy(prior_hbm, prior_ref, sem).start()
        cols = columns()
        for t in range(nt):
            sel_ref[t * width:(t + 1) * width] = (cols[:, t:t + 1] == lanes).astype(BF16)

    out_copies = []

    def finish(t, acc_re, acc_im):
        if has_prior:
            if t == 0:
                pltpu.make_async_copy(prior_hbm, prior_ref, sem).wait()
            acc_re = acc_re + prior_ref[t, 0]
            acc_im = acc_im + prior_ref[t, 1]
        acc_ref[t, 0] = acc_re
        acc_ref[t, 1] = acc_im
        copy = pltpu.make_async_copy(acc_ref.at[t], out_ref.at[t], out_sem.at[t])
        copy.start()
        out_copies.append(copy)

    pending = [(g_ref, k) for g_ref, count in zip(g_refs, counts) for k in range(count)]
    starts = list(range(0, len(pending), CHUNK))
    for start in starts:
        hook = finish if (start == starts[-1] and not final) else None
        add_walkers(pending[start:start + CHUNK], sel_ref, acc_ref, slots, width, hook)
    for copy in out_copies:
        copy.wait()

    @pl.when(w == last)
    def _():
        if not final:
            return
        if has_prior:
            pltpu.make_async_copy(prior_hbm, prior_ref, sem).wait()
        cols = columns()
        q = (cols[:, nt:nt + 1] == lanes).astype(BF16)
        far = far_ref[...]
        partner = [jnp.where(slot_ref[s] == 0, far[2:3], far[3:4]) for s in range(slots)]
        partner = jnp.concatenate(partner + [jnp.zeros((8 - slots, width), jnp.int32)], axis=0)
        partner = lax.dot_general(partner.astype(F32).astype(BF16), q, NT, preferred_element_type=F32)
        levels = jnp.concatenate([ph_ref[...].astype(F32), partner[:slots]], axis=0)
        trig = jnp.concatenate([table(levels, COSINES), table(levels, SINES)], axis=0)
        trig_cols = jnp.concatenate([trig, jnp.zeros((128 - 2 * nt, width), F32)], axis=0).T
        for s in range(slots):
            parts = []
            for t, permute in ((s, False), (s + slots, True)):
                t_re = acc_ref[t, 0] + prior_ref[t, 0] if has_prior else acc_ref[t, 0]
                t_im = acc_ref[t, 1] + prior_ref[t, 1] if has_prior else acc_ref[t, 1]
                if permute:
                    t_re = conj_permuted(q, t_re)
                    t_im = -conj_permuted(q, t_im)
                ca = trig_cols[:, t:t + 1]
                sa = trig_cols[:, nt + t:nt + t + 1]
                cb = trig[t:t + 1]
                sb = trig[nt + t:nt + t + 1]
                rot_re = ca * cb + sa * sb
                rot_im = sa * cb - ca * sb
                parts.append((rot_re * t_re - rot_im * t_im, rot_re * t_im + rot_im * t_re))
            (own_re, own_im), (mir_re, mir_im) = parts
            out_ref[s, 0] = (own_re + mir_re) * scale
            out_ref[s, 1] = (own_im + mir_im) * scale


def walker_spec(width, offset, count):
    return pl.BlockSpec((1, 2, width, width), lambda w: (jnp.clip(w - offset, 0, count - 1), 0, 0, 0))


def accumulate(walkers, info, prior, final, slots, width, scale):
    has_prior = prior is not None
    counts = tuple(g.shape[0] for g in walkers)
    kernel = functools.partial(
        accumulate_kernel, slots=slots, width=width, scale=scale, has_prior=has_prior, final=final, counts=counts
    )
    full = lambda shape: pl.BlockSpec(shape, lambda w: (0,) * len(shape))
    acc_shape = (2 * slots, 2, width, width)
    out_shape = (slots, 2, width, width) if final else acc_shape
    ti, ph, far, slot, cj = info
    in_specs = [full(g.shape) for g in walkers] + [
        full(ti.shape),
        full(ph.shape),
        full(far.shape),
        pl.BlockSpec(memory_space=pltpu.SMEM),
        full(cj.shape),
    ]
    scratch = [pltpu.VMEM(acc_shape, F32), pltpu.VMEM((2 * slots * width, width), BF16)]
    operands = list(walkers) + [ti, ph, far, slot, cj]
    if has_prior:
        in_specs.append(pl.BlockSpec(memory_space=pl.ANY))
        scratch += [pltpu.VMEM(acc_shape, F32), pltpu.SemaphoreType.DMA(())]
        operands.append(prior)
    steps = sum(counts)
    flops = steps * 2 * slots * 8 * width**3 + (8 * slots * 2 * width**3 if final else 0)
    moved = sum(g.size for g in walkers) * 2 + 4 * math.prod(out_shape) + (4 * math.prod(acc_shape) if has_prior else 0)
    return pl.pallas_call(
        kernel,
        grid=(1,),
        cost_estimate=pl.CostEstimate(flops=flops, transcendentals=0, bytes_accessed=moved),
        in_specs=in_specs,
        out_specs=full(out_shape) if final else pl.BlockSpec(memory_space=pl.ANY),
        out_shape=jax.ShapeDtypeStruct(out_shape, F32),
        scratch_shapes=scratch + ([] if final else [pltpu.SemaphoreType.DMA((2 * slots,))]),
        compiler_params=pltpu.CompilerParams(dimension_semantics=("arbitrary",)),
    )(*operands)


def local(greens, transfer_index, phase_index, partner_slot, conj_index):
    slots = transfer_index.shape[0]
    width = greens.shape[-1]
    blocks = lax.axis_size("blk")
    halfway = lax.axis_size("xfer") // 2
    scale = 0.5 / math.sqrt(blocks)
    assert blocks % 2 == 0 and blocks & (blocks - 1) == 0 and 4 * slots + 1 <= 128

    swap = [(i, i ^ 1) for i in range(blocks)]
    sibling = lax.ppermute(greens, "blk", swap)
    fetched = [lax.ppermute(greens, "blk", [(i, i ^ (2 * m)) for i in range(blocks)]) for m in range(1, blocks // 2)]
    far = passed_along(jnp.concatenate([transfer_index, phase_index], axis=0), "xfer", halfway)
    info = (transfer_index, phase_index, far, partner_slot, conj_index.reshape(1, width))
    run = functools.partial(accumulate, info=info, slots=slots, width=width, scale=scale)

    if not fetched:
        return run([greens, sibling], prior=None, final=True)
    partial_sums = run([greens, sibling], prior=None, final=False)
    partial_sums, fetched = lax.optimization_barrier((partial_sums, [fetched[1], fetched[0]] + fetched[2:]))
    near = jnp.concatenate(fetched, axis=0)
    forwarded = lax.ppermute(near, "blk", swap)
    partial_sums = run(fetched, prior=partial_sums, final=False)
    return run([forwarded], prior=partial_sums, final=True)


def solution(mesh):
    in_specs = (
        P("blk", None, None, None),
        P(("blk", "xfer"), None),
        P(("blk", "xfer"), None),
        P(("blk", "xfer")),
        P(),
    )
    out_specs = P(("blk", "xfer"), None, None, None)
    return jax.shard_map(local, mesh=mesh, in_specs=in_specs, out_specs=out_specs, check_vma=False)
```

```python
import functools
import math

import jax
import jax.numpy as jnp
from jax import lax
from jax.experimental import pallas as pl
from jax.experimental.pallas import tpu as pltpu
from jax.sharding import PartitionSpec as P

NPH = 8
F32 = jnp.float32
BF16 = jnp.bfloat16
NT = (((1,), (1,)), ((), ()))
CHUNK = 3
ROOT_HALF = math.sqrt(0.5)
COSINES = (1.0, ROOT_HALF, 0.0, -ROOT_HALF, -1.0, -ROOT_HALF, 0.0, ROOT_HALF)
SINES = (0.0, ROOT_HALF, 1.0, ROOT_HALF, 0.0, -ROOT_HALF, -1.0, -ROOT_HALF)


def passed_along(value, axis, by):
    size = lax.axis_size(axis)
    return lax.ppermute(value, axis, [(i, (i + by) % size) for i in range(size)])


def split2(x):
    hi = x.astype(BF16)
    return (hi, (x - hi.astype(F32)).astype(BF16))


def conj_permuted(q, x):
    total = None
    for piece in split2(x):
        rows = jnp.dot(q, piece, preferred_element_type=F32).astype(BF16)
        moved = lax.dot_general(q, rows, NT, preferred_element_type=F32)
        total = moved if total is None else total + moved
    return total


def table(levels, values):
    out = jnp.zeros(levels.shape, F32)
    for k, v in enumerate(values):
        out = jnp.where(levels == k, v, out)
    return out


def add_walkers(blocks, sel_ref, acc_ref, slots, width, finish=None):
    sel = sel_ref[...]
    terms = []
    for g_ref, k in blocks:
        g_re = g_ref[k, 0]
        g_im = g_ref[k, 1]
        y = jnp.dot(sel, jnp.concatenate([g_re, g_im], axis=1), preferred_element_type=F32).astype(BF16)
        terms.append((g_re.astype(F32), g_im.astype(F32), y))
    for t in range(2 * slots):
        lo, hi = t * width, (t + 1) * width
        acc_re = acc_ref[t, 0]
        acc_im = acc_ref[t, 1]
        for gr, gi, y in terms:
            stacked = jnp.concatenate([y[lo:hi, :width], y[lo:hi, width:]], axis=0)
            m = lax.dot_general(sel[lo:hi], stacked, NT, preferred_element_type=F32)
            m_re = m[:, :width]
            m_im = m[:, width:]
            acc_re = acc_re + (gr * m_re - gi * m_im)
            acc_im = acc_im + (gr * m_im + gi * m_re)
        if finish is None:
            acc_ref[t, 0] = acc_re
            acc_ref[t, 1] = acc_im
        else:
            finish(t, acc_re, acc_im)


def accumulate_kernel(*refs, slots, width, scale, has_prior, final, counts):
    groups = len(counts)
    g_refs = refs[:groups]
    refs = refs[groups:]
    if final:
        refs, out_buf, out_sem = refs[:-2], refs[-2], refs[-1]
    else:
        refs, out_sem = refs[:-1], refs[-1]
    if has_prior:
        (ti_ref, ph_ref, far_ref, slot_ref, cj_ref, prior_hbm, out_ref,
         acc_ref, sel_ref, prior_ref, sem) = refs
    else:
        ti_ref, ph_ref, far_ref, slot_ref, cj_ref, out_ref, acc_ref, sel_ref = refs
    w = pl.program_id(0)
    last = pl.num_programs(0) - 1
    nt = 2 * slots
    lanes = lax.broadcasted_iota(jnp.int32, (width, width), 1).astype(F32)

    def columns():
        far = far_ref[...]
        rows = [ti_ref[pl.ds(s, 1), :] for s in range(slots)]
        for s in range(slots):
            pick = slot_ref[s]
            rows.append(jnp.where(pick == 0, far[0:1], far[1:2]))
        rows.append(cj_ref[...])
        block = jnp.concatenate(rows, axis=0).astype(F32)
        block = jnp.concatenate([block, jnp.zeros((128 - block.shape[0], width), F32)], axis=0)
        return block.T

    @pl.when(w == 0)
    def _():
        acc_ref[...] = jnp.zeros(acc_ref.shape, F32)
        if has_prior:
            pltpu.make_async_copy(prior_hbm, prior_ref, sem).start()
        cols = columns()
        for t in range(nt):
            sel_ref[t * width:(t + 1) * width] = (cols[:, t:t + 1] == lanes).astype(BF16)

    out_copies = []

    def finish(t, acc_re, acc_im):
        if has_prior:
            if t == 0:
                pltpu.make_async_copy(prior_hbm, prior_ref, sem).wait()
            acc_re = acc_re + prior_ref[t, 0]
            acc_im = acc_im + prior_ref[t, 1]
        acc_ref[t, 0] = acc_re
        acc_ref[t, 1] = acc_im
        copy = pltpu.make_async_copy(acc_ref.at[t], out_ref.at[t], out_sem.at[t])
        copy.start()
        out_copies.append(copy)

    pending = [(g_ref, k) for g_ref, count in zip(g_refs, counts) for k in range(count)]
    starts = list(range(0, len(pending), CHUNK))
    for start in starts:
        hook = finish if (start == starts[-1] and not final) else None
        add_walkers(pending[start:start + CHUNK], sel_ref, acc_ref, slots, width, hook)
    for copy in out_copies:
        copy.wait()

    @pl.when(w == last)
    def _():
        if not final:
            return
        if has_prior:
            pltpu.make_async_copy(prior_hbm, prior_ref, sem).wait()
        cols = columns()
        q = (cols[:, nt:nt + 1] == lanes).astype(BF16)
        sent = []
        far = far_ref[...]
        partner = [jnp.where(slot_ref[s] == 0, far[2:3], far[3:4]) for s in range(slots)]
        partner = jnp.concatenate(partner + [jnp.zeros((8 - slots, width), jnp.int32)], axis=0)
        partner = lax.dot_general(partner.astype(F32).astype(BF16), q, NT, preferred_element_type=F32)
        levels = jnp.concatenate([ph_ref[...].astype(F32), partner[:slots]], axis=0)
        trig = jnp.concatenate([table(levels, COSINES), table(levels, SINES)], axis=0)
        trig_cols = jnp.concatenate([trig, jnp.zeros((128 - 2 * nt, width), F32)], axis=0).T
        for s in range(slots):
            parts = []
            for t, permute in ((s, False), (s + slots, True)):
                t_re = acc_ref[t, 0] + prior_ref[t, 0] if has_prior else acc_ref[t, 0]
                t_im = acc_ref[t, 1] + prior_ref[t, 1] if has_prior else acc_ref[t, 1]
                if permute:
                    t_re = conj_permuted(q, t_re)
                    t_im = -conj_permuted(q, t_im)
                ca = trig_cols[:, t:t + 1] * scale
                sa = trig_cols[:, nt + t:nt + t + 1] * scale
                cb = trig[t:t + 1]
                sb = trig[nt + t:nt + t + 1]
                rot_re = ca * cb + sa * sb
                rot_im = sa * cb - ca * sb
                parts.append((rot_re * t_re - rot_im * t_im, rot_re * t_im + rot_im * t_re))
            (own_re, own_im), (mir_re, mir_im) = parts
            out_buf[s, 0] = own_re + mir_re
            out_buf[s, 1] = own_im + mir_im
            copy = pltpu.make_async_copy(out_buf.at[s], out_ref.at[s], out_sem.at[s])
            copy.start()
            sent.append(copy)
        for copy in sent:
            copy.wait()


def walker_spec(width, offset, count):
    return pl.BlockSpec((1, 2, width, width), lambda w: (jnp.clip(w - offset, 0, count - 1), 0, 0, 0))


def accumulate(walkers, info, prior, final, slots, width, scale):
    has_prior = prior is not None
    counts = tuple(g.shape[0] for g in walkers)
    kernel = functools.partial(
        accumulate_kernel, slots=slots, width=width, scale=scale, has_prior=has_prior, final=final, counts=counts
    )
    full = lambda shape: pl.BlockSpec(shape, lambda w: (0,) * len(shape))
    acc_shape = (2 * slots, 2, width, width)
    out_shape = (slots, 2, width, width) if final else acc_shape
    ti, ph, far, slot, cj = info
    in_specs = [full(g.shape) for g in walkers] + [
        full(ti.shape),
        full(ph.shape),
        full(far.shape),
        pl.BlockSpec(memory_space=pltpu.SMEM),
        full(cj.shape),
    ]
    scratch = [pltpu.VMEM(acc_shape, F32), pltpu.VMEM((2 * slots * width, width), BF16)]
    operands = list(walkers) + [ti, ph, far, slot, cj]
    if has_prior:
        in_specs.append(pl.BlockSpec(memory_space=pl.ANY))
        scratch += [pltpu.VMEM(acc_shape, F32), pltpu.SemaphoreType.DMA(())]
        operands.append(prior)
    steps = sum(counts)
    flops = steps * 2 * slots * 8 * width**3 + (8 * slots * 2 * width**3 if final else 0)
    moved = sum(g.size for g in walkers) * 2 + 4 * math.prod(out_shape) + (4 * math.prod(acc_shape) if has_prior else 0)
    return pl.pallas_call(
        kernel,
        grid=(1,),
        cost_estimate=pl.CostEstimate(flops=flops, transcendentals=0, bytes_accessed=moved),
        in_specs=in_specs,
        out_specs=pl.BlockSpec(memory_space=pl.ANY),
        out_shape=jax.ShapeDtypeStruct(out_shape, F32),
        scratch_shapes=scratch + (
            [pltpu.VMEM(out_shape, F32), pltpu.SemaphoreType.DMA((slots,))]
            if final
            else [pltpu.SemaphoreType.DMA((2 * slots,))]
        ),
        compiler_params=pltpu.CompilerParams(dimension_semantics=("arbitrary",)),
    )(*operands)


def local(greens, transfer_index, phase_index, partner_slot, conj_index):
    slots = transfer_index.shape[0]
    width = greens.shape[-1]
    blocks = lax.axis_size("blk")
    halfway = lax.axis_size("xfer") // 2
    scale = 0.5 / math.sqrt(blocks)
    assert blocks % 2 == 0 and blocks & (blocks - 1) == 0 and 4 * slots + 1 <= 128

    swap = [(i, i ^ 1) for i in range(blocks)]
    sibling = lax.ppermute(greens, "blk", swap)
    fetched = [lax.ppermute(greens, "blk", [(i, i ^ (2 * m)) for i in range(blocks)]) for m in range(1, blocks // 2)]
    far = passed_along(jnp.concatenate([transfer_index, phase_index], axis=0), "xfer", halfway)
    info = (transfer_index, phase_index, far, partner_slot, conj_index.reshape(1, width))
    run = functools.partial(accumulate, info=info, slots=slots, width=width, scale=scale)

    if not fetched:
        return run([greens, sibling], prior=None, final=True)
    partial_sums = run([greens, sibling], prior=None, final=False)
    partial_sums, fetched = lax.optimization_barrier((partial_sums, [fetched[1], fetched[0]] + fetched[2:]))
    near = jnp.concatenate(fetched, axis=0)
    forwarded = lax.ppermute(near, "blk", swap)
    partial_sums = run(fetched, prior=partial_sums, final=False)
    return run([forwarded], prior=partial_sums, final=True)


def solution(mesh):
    in_specs = (
        P("blk", None, None, None),
        P(("blk", "xfer"), None),
        P(("blk", "xfer"), None),
        P(("blk", "xfer")),
        P(),
    )
    out_specs = P(("blk", "xfer"), None, None, None)
    return jax.shard_map(local, mesh=mesh, in_specs=in_specs, out_specs=out_specs, check_vma=False)
```

```python
import functools
import math

import jax
import jax.numpy as jnp
from jax import lax
from jax.experimental import pallas as pl
from jax.experimental.pallas import tpu as pltpu
from jax.sharding import PartitionSpec as P

NPH = 8
F32 = jnp.float32
BF16 = jnp.bfloat16
NT = (((1,), (1,)), ((), ()))
CHUNK = 2
ROOT_HALF = math.sqrt(0.5)
COSINES = (1.0, ROOT_HALF, 0.0, -ROOT_HALF, -1.0, -ROOT_HALF, 0.0, ROOT_HALF)
SINES = (0.0, ROOT_HALF, 1.0, ROOT_HALF, 0.0, -ROOT_HALF, -1.0, -ROOT_HALF)


def passed_along(value, axis, by):
    size = lax.axis_size(axis)
    return lax.ppermute(value, axis, [(i, (i + by) % size) for i in range(size)])


def split2(x):
    hi = x.astype(BF16)
    return (hi, (x - hi.astype(F32)).astype(BF16))


def conj_permuted(q, x):
    total = None
    for piece in split2(x):
        rows = jnp.dot(q, piece, preferred_element_type=F32).astype(BF16)
        moved = lax.dot_general(q, rows, NT, preferred_element_type=F32)
        total = moved if total is None else total + moved
    return total


def table(levels, values):
    out = jnp.zeros(levels.shape, F32)
    for k, v in enumerate(values):
        out = jnp.where(levels == k, v, out)
    return out


def add_walkers(blocks, sel_ref, acc_ref, slots, width, finish=None):
    sel = sel_ref[...]
    terms = []
    for g_ref, k in blocks:
        g_re = g_ref[k, 0]
        g_im = g_ref[k, 1]
        y = jnp.dot(sel, jnp.concatenate([g_re, g_im], axis=1), preferred_element_type=F32).astype(BF16)
        terms.append((g_re.astype(F32), g_im.astype(F32), y))
    for t in range(2 * slots):
        lo, hi = t * width, (t + 1) * width
        acc_re = acc_ref[t, 0]
        acc_im = acc_ref[t, 1]
        for gr, gi, y in terms:
            stacked = jnp.concatenate([y[lo:hi, :width], y[lo:hi, width:]], axis=0)
            m = lax.dot_general(sel[lo:hi], stacked, NT, preferred_element_type=F32)
            m_re = m[:, :width]
            m_im = m[:, width:]
            acc_re = acc_re + (gr * m_re - gi * m_im)
            acc_im = acc_im + (gr * m_im + gi * m_re)
        if finish is None:
            acc_ref[t, 0] = acc_re
            acc_ref[t, 1] = acc_im
        else:
            finish(t, acc_re, acc_im)


def accumulate_kernel(*refs, slots, width, scale, has_prior, final, counts):
    groups = len(counts)
    g_refs = refs[:groups]
    refs = refs[groups:]
    if final:
        refs, out_buf, out_sem = refs[:-2], refs[-2], refs[-1]
    else:
        refs, out_sem = refs[:-1], refs[-1]
    if has_prior:
        (ti_ref, ph_ref, far_ref, slot_ref, cj_ref, prior_hbm, out_ref,
         acc_ref, sel_ref, prior_ref, sem) = refs
    else:
        ti_ref, ph_ref, far_ref, slot_ref, cj_ref, out_ref, acc_ref, sel_ref = refs
    w = pl.program_id(0)
    last = pl.num_programs(0) - 1
    nt = 2 * slots
    lanes = lax.broadcasted_iota(jnp.int32, (width, width), 1).astype(F32)

    def columns():
        far = far_ref[...]
        rows = [ti_ref[pl.ds(s, 1), :] for s in range(slots)]
        for s in range(slots):
            pick = slot_ref[s]
            rows.append(jnp.where(pick == 0, far[0:1], far[1:2]))
        rows.append(cj_ref[...])
        block = jnp.concatenate(rows, axis=0).astype(F32)
        block = jnp.concatenate([block, jnp.zeros((128 - block.shape[0], width), F32)], axis=0)
        return block.T

    @pl.when(w == 0)
    def _():
        acc_ref[...] = jnp.zeros(acc_ref.shape, F32)
        if has_prior:
            pltpu.make_async_copy(prior_hbm, prior_ref, sem).start()
        cols = columns()
        for t in range(nt):
            sel_ref[t * width:(t + 1) * width] = (cols[:, t:t + 1] == lanes).astype(BF16)

    out_copies = []

    def finish(t, acc_re, acc_im):
        if has_prior:
            if t == 0:
                pltpu.make_async_copy(prior_hbm, prior_ref, sem).wait()
            acc_re = acc_re + prior_ref[t, 0]
            acc_im = acc_im + prior_ref[t, 1]
        acc_ref[t, 0] = acc_re
        acc_ref[t, 1] = acc_im
        copy = pltpu.make_async_copy(acc_ref.at[t], out_ref.at[t], out_sem.at[t])
        copy.start()
        out_copies.append(copy)

    pending = [(g_ref, k) for g_ref, count in zip(g_refs, counts) for k in range(count)]
    starts = list(range(0, len(pending), CHUNK))
    for start in starts:
        hook = finish if (start == starts[-1] and not final) else None
        add_walkers(pending[start:start + CHUNK], sel_ref, acc_ref, slots, width, hook)
    for copy in out_copies:
        copy.wait()

    @pl.when(w == last)
    def _():
        if not final:
            return
        if has_prior:
            pltpu.make_async_copy(prior_hbm, prior_ref, sem).wait()
        cols = columns()
        q = (cols[:, nt:nt + 1] == lanes).astype(BF16)
        sent = []
        far = far_ref[...]
        partner = [jnp.where(slot_ref[s] == 0, far[2:3], far[3:4]) for s in range(slots)]
        partner = jnp.concatenate(partner + [jnp.zeros((8 - slots, width), jnp.int32)], axis=0)
        partner = lax.dot_general(partner.astype(F32).astype(BF16), q, NT, preferred_element_type=F32)
        levels = jnp.concatenate([ph_ref[...].astype(F32), partner[:slots]], axis=0)
        trig = jnp.concatenate([table(levels, COSINES), table(levels, SINES)], axis=0)
        trig_cols = jnp.concatenate([trig, jnp.zeros((128 - 2 * nt, width), F32)], axis=0).T
        for s in range(slots):
            parts = []
            for t, permute in ((s, False), (s + slots, True)):
                t_re = acc_ref[t, 0] + prior_ref[t, 0] if has_prior else acc_ref[t, 0]
                t_im = acc_ref[t, 1] + prior_ref[t, 1] if has_prior else acc_ref[t, 1]
                if permute:
                    t_re = conj_permuted(q, t_re)
                    t_im = -conj_permuted(q, t_im)
                ca = trig_cols[:, t:t + 1] * scale
                sa = trig_cols[:, nt + t:nt + t + 1] * scale
                cb = trig[t:t + 1]
                sb = trig[nt + t:nt + t + 1]
                rot_re = ca * cb + sa * sb
                rot_im = sa * cb - ca * sb
                parts.append((rot_re * t_re - rot_im * t_im, rot_re * t_im + rot_im * t_re))
            (own_re, own_im), (mir_re, mir_im) = parts
            out_buf[s, 0] = own_re + mir_re
            out_buf[s, 1] = own_im + mir_im
            copy = pltpu.make_async_copy(out_buf.at[s], out_ref.at[s], out_sem.at[s])
            copy.start()
            sent.append(copy)
        for copy in sent:
            copy.wait()


def walker_spec(width, offset, count):
    return pl.BlockSpec((1, 2, width, width), lambda w: (jnp.clip(w - offset, 0, count - 1), 0, 0, 0))


def accumulate(walkers, info, prior, final, slots, width, scale):
    has_prior = prior is not None
    counts = tuple(g.shape[0] for g in walkers)
    kernel = functools.partial(
        accumulate_kernel, slots=slots, width=width, scale=scale, has_prior=has_prior, final=final, counts=counts
    )
    full = lambda shape: pl.BlockSpec(shape, lambda w: (0,) * len(shape))
    acc_shape = (2 * slots, 2, width, width)
    out_shape = (slots, 2, width, width) if final else acc_shape
    ti, ph, far, slot, cj = info
    in_specs = [full(g.shape) for g in walkers] + [
        full(ti.shape),
        full(ph.shape),
        full(far.shape),
        pl.BlockSpec(memory_space=pltpu.SMEM),
        full(cj.shape),
    ]
    scratch = [pltpu.VMEM(acc_shape, F32), pltpu.VMEM((2 * slots * width, width), BF16)]
    operands = list(walkers) + [ti, ph, far, slot, cj]
    if has_prior:
        in_specs.append(pl.BlockSpec(memory_space=pl.ANY))
        scratch += [pltpu.VMEM(acc_shape, F32), pltpu.SemaphoreType.DMA(())]
        operands.append(prior)
    steps = sum(counts)
    flops = steps * 2 * slots * 8 * width**3 + (8 * slots * 2 * width**3 if final else 0)
    moved = sum(g.size for g in walkers) * 2 + 4 * math.prod(out_shape) + (4 * math.prod(acc_shape) if has_prior else 0)
    return pl.pallas_call(
        kernel,
        grid=(1,),
        cost_estimate=pl.CostEstimate(flops=flops, transcendentals=0, bytes_accessed=moved),
        in_specs=in_specs,
        out_specs=pl.BlockSpec(memory_space=pl.ANY),
        out_shape=jax.ShapeDtypeStruct(out_shape, F32),
        scratch_shapes=scratch + (
            [pltpu.VMEM(out_shape, F32), pltpu.SemaphoreType.DMA((slots,))]
            if final
            else [pltpu.SemaphoreType.DMA((2 * slots,))]
        ),
        compiler_params=pltpu.CompilerParams(dimension_semantics=("arbitrary",)),
    )(*operands)


def local(greens, transfer_index, phase_index, partner_slot, conj_index):
    slots = transfer_index.shape[0]
    width = greens.shape[-1]
    blocks = lax.axis_size("blk")
    halfway = lax.axis_size("xfer") // 2
    scale = 0.5 / math.sqrt(blocks)
    assert blocks % 2 == 0 and blocks & (blocks - 1) == 0 and 4 * slots + 1 <= 128

    swap = [(i, i ^ 1) for i in range(blocks)]
    sibling = lax.ppermute(greens, "blk", swap)
    fetched = [lax.ppermute(greens, "blk", [(i, i ^ (2 * m)) for i in range(blocks)]) for m in range(1, blocks // 2)]
    far = passed_along(jnp.concatenate([transfer_index, phase_index], axis=0), "xfer", halfway)
    info = (transfer_index, phase_index, far, partner_slot, conj_index.reshape(1, width))
    run = functools.partial(accumulate, info=info, slots=slots, width=width, scale=scale)

    if not fetched:
        return run([greens, sibling], prior=None, final=True)
    partial_sums = run([greens, sibling], prior=None, final=False)
    partial_sums, fetched = lax.optimization_barrier((partial_sums, [fetched[1], fetched[0]] + fetched[2:]))
    near = jnp.concatenate(fetched, axis=0)
    forwarded = lax.ppermute(near, "blk", swap)
    partial_sums = run(fetched, prior=partial_sums, final=False)
    return run([forwarded], prior=partial_sums, final=True)


def solution(mesh):
    in_specs = (
        P("blk", None, None, None),
        P(("blk", "xfer"), None),
        P(("blk", "xfer"), None),
        P(("blk", "xfer")),
        P(),
    )
    out_specs = P(("blk", "xfer"), None, None, None)
    return jax.shard_map(local, mesh=mesh, in_specs=in_specs, out_specs=out_specs, check_vma=False)
```

```python
import functools
import math

import jax
import jax.numpy as jnp
from jax import lax
from jax.experimental import pallas as pl
from jax.experimental.pallas import tpu as pltpu
from jax.sharding import PartitionSpec as P

NPH = 8
F32 = jnp.float32
BF16 = jnp.bfloat16
NT = (((1,), (1,)), ((), ()))
CHUNK = 1
ROOT_HALF = math.sqrt(0.5)
COSINES = (1.0, ROOT_HALF, 0.0, -ROOT_HALF, -1.0, -ROOT_HALF, 0.0, ROOT_HALF)
SINES = (0.0, ROOT_HALF, 1.0, ROOT_HALF, 0.0, -ROOT_HALF, -1.0, -ROOT_HALF)


def passed_along(value, axis, by):
    size = lax.axis_size(axis)
    return lax.ppermute(value, axis, [(i, (i + by) % size) for i in range(size)])


def split2(x):
    hi = x.astype(BF16)
    return (hi, (x - hi.astype(F32)).astype(BF16))


def conj_permuted(q, x):
    total = None
    for piece in split2(x):
        rows = jnp.dot(q, piece, preferred_element_type=F32).astype(BF16)
        moved = lax.dot_general(q, rows, NT, preferred_element_type=F32)
        total = moved if total is None else total + moved
    return total


def table(levels, values):
    out = jnp.zeros(levels.shape, F32)
    for k, v in enumerate(values):
        out = jnp.where(levels == k, v, out)
    return out


def add_walkers(blocks, sel_ref, acc_ref, slots, width, finish=None):
    sel = sel_ref[...]
    terms = []
    for g_ref, k in blocks:
        g_re = g_ref[k, 0]
        g_im = g_ref[k, 1]
        y = jnp.dot(sel, jnp.concatenate([g_re, g_im], axis=1), preferred_element_type=F32).astype(BF16)
        terms.append((g_re.astype(F32), g_im.astype(F32), y))
    for t in range(2 * slots):
        lo, hi = t * width, (t + 1) * width
        acc_re = acc_ref[t, 0]
        acc_im = acc_ref[t, 1]
        for gr, gi, y in terms:
            stacked = jnp.concatenate([y[lo:hi, :width], y[lo:hi, width:]], axis=0)
            m = lax.dot_general(sel[lo:hi], stacked, NT, preferred_element_type=F32)
            m_re = m[:, :width]
            m_im = m[:, width:]
            acc_re = acc_re + (gr * m_re - gi * m_im)
            acc_im = acc_im + (gr * m_im + gi * m_re)
        if finish is None:
            acc_ref[t, 0] = acc_re
            acc_ref[t, 1] = acc_im
        else:
            finish(t, acc_re, acc_im)


def accumulate_kernel(*refs, slots, width, scale, has_prior, final, counts):
    groups = len(counts)
    g_refs = refs[:groups]
    refs = refs[groups:]
    if final:
        refs, out_buf, out_sem = refs[:-2], refs[-2], refs[-1]
    else:
        refs, out_sem = refs[:-1], refs[-1]
    if has_prior:
        (ti_ref, ph_ref, far_ref, slot_ref, cj_ref, prior_hbm, out_ref,
         acc_ref, sel_ref, prior_ref, sem) = refs
    else:
        ti_ref, ph_ref, far_ref, slot_ref, cj_ref, out_ref, acc_ref, sel_ref = refs
    w = pl.program_id(0)
    last = pl.num_programs(0) - 1
    nt = 2 * slots
    lanes = lax.broadcasted_iota(jnp.int32, (width, width), 1).astype(F32)

    def columns():
        far = far_ref[...]
        rows = [ti_ref[pl.ds(s, 1), :] for s in range(slots)]
        for s in range(slots):
            pick = slot_ref[s]
            rows.append(jnp.where(pick == 0, far[0:1], far[1:2]))
        rows.append(cj_ref[...])
        block = jnp.concatenate(rows, axis=0).astype(F32)
        block = jnp.concatenate([block, jnp.zeros((128 - block.shape[0], width), F32)], axis=0)
        return block.T

    @pl.when(w == 0)
    def _():
        acc_ref[...] = jnp.zeros(acc_ref.shape, F32)
        if has_prior:
            pltpu.make_async_copy(prior_hbm, prior_ref, sem).start()
        cols = columns()
        for t in range(nt):
            sel_ref[t * width:(t + 1) * width] = (cols[:, t:t + 1] == lanes).astype(BF16)

    out_copies = []

    def finish(t, acc_re, acc_im):
        if has_prior:
            if t == 0:
                pltpu.make_async_copy(prior_hbm, prior_ref, sem).wait()
            acc_re = acc_re + prior_ref[t, 0]
            acc_im = acc_im + prior_ref[t, 1]
        acc_ref[t, 0] = acc_re
        acc_ref[t, 1] = acc_im
        copy = pltpu.make_async_copy(acc_ref.at[t], out_ref.at[t], out_sem.at[t])
        copy.start()
        out_copies.append(copy)

    pending = [(g_ref, k) for g_ref, count in zip(g_refs, counts) for k in range(count)]
    starts = list(range(0, len(pending), CHUNK))
    for start in starts:
        hook = finish if (start == starts[-1] and not final) else None
        add_walkers(pending[start:start + CHUNK], sel_ref, acc_ref, slots, width, hook)
    for copy in out_copies:
        copy.wait()

    @pl.when(w == last)
    def _():
        if not final:
            return
        if has_prior:
            pltpu.make_async_copy(prior_hbm, prior_ref, sem).wait()
        cols = columns()
        q = (cols[:, nt:nt + 1] == lanes).astype(BF16)
        sent = []
        far = far_ref[...]
        partner = [jnp.where(slot_ref[s] == 0, far[2:3], far[3:4]) for s in range(slots)]
        partner = jnp.concatenate(partner + [jnp.zeros((8 - slots, width), jnp.int32)], axis=0)
        partner = lax.dot_general(partner.astype(F32).astype(BF16), q, NT, preferred_element_type=F32)
        levels = jnp.concatenate([ph_ref[...].astype(F32), partner[:slots]], axis=0)
        trig = jnp.concatenate([table(levels, COSINES), table(levels, SINES)], axis=0)
        trig_cols = jnp.concatenate([trig, jnp.zeros((128 - 2 * nt, width), F32)], axis=0).T
        for s in range(slots):
            parts = []
            for t, permute in ((s, False), (s + slots, True)):
                t_re = acc_ref[t, 0] + prior_ref[t, 0] if has_prior else acc_ref[t, 0]
                t_im = acc_ref[t, 1] + prior_ref[t, 1] if has_prior else acc_ref[t, 1]
                if permute:
                    t_re = conj_permuted(q, t_re)
                    t_im = -conj_permuted(q, t_im)
                ca = trig_cols[:, t:t + 1] * scale
                sa = trig_cols[:, nt + t:nt + t + 1] * scale
                cb = trig[t:t + 1]
                sb = trig[nt + t:nt + t + 1]
                rot_re = ca * cb + sa * sb
                rot_im = sa * cb - ca * sb
                parts.append((rot_re * t_re - rot_im * t_im, rot_re * t_im + rot_im * t_re))
            (own_re, own_im), (mir_re, mir_im) = parts
            out_buf[s, 0] = own_re + mir_re
            out_buf[s, 1] = own_im + mir_im
            copy = pltpu.make_async_copy(out_buf.at[s], out_ref.at[s], out_sem.at[s])
            copy.start()
            sent.append(copy)
        for copy in sent:
            copy.wait()


def walker_spec(width, offset, count):
    return pl.BlockSpec((1, 2, width, width), lambda w: (jnp.clip(w - offset, 0, count - 1), 0, 0, 0))


def accumulate(walkers, info, prior, final, slots, width, scale):
    has_prior = prior is not None
    counts = tuple(g.shape[0] for g in walkers)
    kernel = functools.partial(
        accumulate_kernel, slots=slots, width=width, scale=scale, has_prior=has_prior, final=final, counts=counts
    )
    full = lambda shape: pl.BlockSpec(shape, lambda w: (0,) * len(shape))
    acc_shape = (2 * slots, 2, width, width)
    out_shape = (slots, 2, width, width) if final else acc_shape
    ti, ph, far, slot, cj = info
    in_specs = [full(g.shape) for g in walkers] + [
        full(ti.shape),
        full(ph.shape),
        full(far.shape),
        pl.BlockSpec(memory_space=pltpu.SMEM),
        full(cj.shape),
    ]
    scratch = [pltpu.VMEM(acc_shape, F32), pltpu.VMEM((2 * slots * width, width), BF16)]
    operands = list(walkers) + [ti, ph, far, slot, cj]
    if has_prior:
        in_specs.append(pl.BlockSpec(memory_space=pl.ANY))
        scratch += [pltpu.VMEM(acc_shape, F32), pltpu.SemaphoreType.DMA(())]
        operands.append(prior)
    steps = sum(counts)
    flops = steps * 2 * slots * 8 * width**3 + (8 * slots * 2 * width**3 if final else 0)
    moved = sum(g.size for g in walkers) * 2 + 4 * math.prod(out_shape) + (4 * math.prod(acc_shape) if has_prior else 0)
    return pl.pallas_call(
        kernel,
        grid=(1,),
        cost_estimate=pl.CostEstimate(flops=flops, transcendentals=0, bytes_accessed=moved),
        in_specs=in_specs,
        out_specs=pl.BlockSpec(memory_space=pl.ANY),
        out_shape=jax.ShapeDtypeStruct(out_shape, F32),
        scratch_shapes=scratch + (
            [pltpu.VMEM(out_shape, F32), pltpu.SemaphoreType.DMA((slots,))]
            if final
            else [pltpu.SemaphoreType.DMA((2 * slots,))]
        ),
        compiler_params=pltpu.CompilerParams(dimension_semantics=("arbitrary",)),
    )(*operands)


def local(greens, transfer_index, phase_index, partner_slot, conj_index):
    slots = transfer_index.shape[0]
    width = greens.shape[-1]
    blocks = lax.axis_size("blk")
    halfway = lax.axis_size("xfer") // 2
    scale = 0.5 / math.sqrt(blocks)
    assert blocks % 2 == 0 and blocks & (blocks - 1) == 0 and 4 * slots + 1 <= 128

    swap = [(i, i ^ 1) for i in range(blocks)]
    sibling = lax.ppermute(greens, "blk", swap)
    fetched = [lax.ppermute(greens, "blk", [(i, i ^ (2 * m)) for i in range(blocks)]) for m in range(1, blocks // 2)]
    far = passed_along(jnp.concatenate([transfer_index, phase_index], axis=0), "xfer", halfway)
    info = (transfer_index, phase_index, far, partner_slot, conj_index.reshape(1, width))
    run = functools.partial(accumulate, info=info, slots=slots, width=width, scale=scale)

    if not fetched:
        return run([greens, sibling], prior=None, final=True)
    partial_sums = run([greens, sibling], prior=None, final=False)
    partial_sums, fetched = lax.optimization_barrier((partial_sums, [fetched[1], fetched[0]] + fetched[2:]))
    near = jnp.concatenate(fetched, axis=0)
    forwarded = lax.ppermute(near, "blk", swap)
    partial_sums = run(fetched, prior=partial_sums, final=False)
    return run([forwarded], prior=partial_sums, final=True)


def solution(mesh):
    in_specs = (
        P("blk", None, None, None),
        P(("blk", "xfer"), None),
        P(("blk", "xfer"), None),
        P(("blk", "xfer")),
        P(),
    )
    out_specs = P(("blk", "xfer"), None, None, None)
    return jax.shard_map(local, mesh=mesh, in_specs=in_specs, out_specs=out_specs, check_vma=False)
```

```python
import functools
import math

import jax
import jax.numpy as jnp
from jax import lax
from jax.experimental import pallas as pl
from jax.experimental.pallas import tpu as pltpu
from jax.sharding import PartitionSpec as P

NPH = 8
F32 = jnp.float32
BF16 = jnp.bfloat16
NT = (((1,), (1,)), ((), ()))
CHUNK = 1
ROOT_HALF = math.sqrt(0.5)
COSINES = (1.0, ROOT_HALF, 0.0, -ROOT_HALF, -1.0, -ROOT_HALF, 0.0, ROOT_HALF)
SINES = (0.0, ROOT_HALF, 1.0, ROOT_HALF, 0.0, -ROOT_HALF, -1.0, -ROOT_HALF)


def passed_along(value, axis, by):
    size = lax.axis_size(axis)
    return lax.ppermute(value, axis, [(i, (i + by) % size) for i in range(size)])


def split2(x):
    hi = x.astype(BF16)
    return (hi, (x - hi.astype(F32)).astype(BF16))


def conj_permuted(q, x):
    total = None
    for piece in split2(x):
        rows = jnp.dot(q, piece, preferred_element_type=F32).astype(BF16)
        moved = lax.dot_general(q, rows, NT, preferred_element_type=F32)
        total = moved if total is None else total + moved
    return total


def table(levels, values):
    out = jnp.zeros(levels.shape, F32)
    for k, v in enumerate(values):
        out = jnp.where(levels == k, v, out)
    return out


def add_walkers(blocks, sel_ref, acc_ref, slots, width, finish=None):
    sel = sel_ref[...]
    terms = []
    for g_ref, k in blocks:
        g_re = g_ref[k, 0]
        g_im = g_ref[k, 1]
        y = jnp.dot(sel, jnp.concatenate([g_re, g_im], axis=1), preferred_element_type=F32).astype(BF16)
        terms.append((g_re.astype(F32), g_im.astype(F32), y))
    for t in range(2 * slots):
        lo, hi = t * width, (t + 1) * width
        acc_re = acc_ref[t, 0]
        acc_im = acc_ref[t, 1]
        for gr, gi, y in terms:
            stacked = jnp.concatenate([y[lo:hi, :width], y[lo:hi, width:]], axis=0)
            m = lax.dot_general(sel[lo:hi], stacked, NT, preferred_element_type=F32)
            m_re = m[:, :width]
            m_im = m[:, width:]
            acc_re = acc_re + (gr * m_re - gi * m_im)
            acc_im = acc_im + (gr * m_im + gi * m_re)
        if finish is None:
            acc_ref[t, 0] = acc_re
            acc_ref[t, 1] = acc_im
        else:
            finish(t, acc_re, acc_im)


def accumulate_kernel(*refs, slots, width, scale, has_prior, final, counts):
    groups = len(counts)
    g_refs = refs[:groups]
    refs = refs[groups:]
    if final:
        refs, out_buf, out_sem = refs[:-2], refs[-2], refs[-1]
    else:
        refs, out_sem = refs[:-1], refs[-1]
    if has_prior:
        (ti_ref, ph_ref, far_ref, slot_ref, cj_ref, prior_hbm, out_ref,
         acc_ref, sel_ref, prior_ref, sem) = refs
    else:
        ti_ref, ph_ref, far_ref, slot_ref, cj_ref, out_ref, acc_ref, sel_ref = refs
    w = pl.program_id(0)
    last = pl.num_programs(0) - 1
    nt = 2 * slots
    lanes = lax.broadcasted_iota(jnp.int32, (width, width), 1).astype(F32)

    def columns():
        far = far_ref[...]
        rows = [ti_ref[pl.ds(s, 1), :] for s in range(slots)]
        for s in range(slots):
            pick = slot_ref[s]
            rows.append(jnp.where(pick == 0, far[0:1], far[1:2]))
        rows.append(cj_ref[...])
        block = jnp.concatenate(rows, axis=0).astype(F32)
        block = jnp.concatenate([block, jnp.zeros((128 - block.shape[0], width), F32)], axis=0)
        return block.T

    @pl.when(w == 0)
    def _():
        acc_ref[...] = jnp.zeros(acc_ref.shape, F32)
        if has_prior:
            pltpu.make_async_copy(prior_hbm, prior_ref, sem).start()
        cols = columns()
        for t in range(nt):
            sel_ref[t * width:(t + 1) * width] = (cols[:, t:t + 1] == lanes).astype(BF16)

    out_copies = []

    def finish(t, acc_re, acc_im):
        if has_prior:
            if t == 0:
                pltpu.make_async_copy(prior_hbm, prior_ref, sem).wait()
            acc_re = acc_re + prior_ref[t, 0]
            acc_im = acc_im + prior_ref[t, 1]
        acc_ref[t, 0] = acc_re
        acc_ref[t, 1] = acc_im
        copy = pltpu.make_async_copy(acc_ref.at[t], out_ref.at[t], out_sem.at[t])
        copy.start()
        out_copies.append(copy)

    pending = [(g_ref, k) for g_ref, count in zip(g_refs, counts) for k in range(count)]
    starts = list(range(0, len(pending), CHUNK))
    for start in starts:
        hook = finish if (start == starts[-1] and not final) else None
        add_walkers(pending[start:start + CHUNK], sel_ref, acc_ref, slots, width, hook)
    for copy in out_copies:
        copy.wait()

    @pl.when(w == last)
    def _():
        if not final:
            return
        if has_prior:
            pltpu.make_async_copy(prior_hbm, prior_ref, sem).wait()
        cols = columns()
        q = (cols[:, nt:nt + 1] == lanes).astype(BF16)
        sent = []
        far = far_ref[...]
        partner = [jnp.where(slot_ref[s] == 0, far[2:3], far[3:4]) for s in range(slots)]
        partner = jnp.concatenate(partner + [jnp.zeros((8 - slots, width), jnp.int32)], axis=0)
        partner = lax.dot_general(partner.astype(F32).astype(BF16), q, NT, preferred_element_type=F32)
        levels = jnp.concatenate([ph_ref[...].astype(F32), partner[:slots]], axis=0)
        trig = jnp.concatenate([table(levels, COSINES), table(levels, SINES)], axis=0)
        trig_cols = jnp.concatenate([trig, jnp.zeros((128 - 2 * nt, width), F32)], axis=0).T
        for s in range(slots):
            parts = []
            for t, permute in ((s, False), (s + slots, True)):
                t_re = acc_ref[t, 0] + prior_ref[t, 0] if has_prior else acc_ref[t, 0]
                t_im = acc_ref[t, 1] + prior_ref[t, 1] if has_prior else acc_ref[t, 1]
                if permute:
                    t_re = conj_permuted(q, t_re)
                    t_im = -conj_permuted(q, t_im)
                ca = trig_cols[:, t:t + 1] * scale
                sa = trig_cols[:, nt + t:nt + t + 1] * scale
                cb = trig[t:t + 1]
                sb = trig[nt + t:nt + t + 1]
                rot_re = ca * cb + sa * sb
                rot_im = sa * cb - ca * sb
                parts.append((rot_re * t_re - rot_im * t_im, rot_re * t_im + rot_im * t_re))
            (own_re, own_im), (mir_re, mir_im) = parts
            out_buf[s, 0] = own_re + mir_re
            out_buf[s, 1] = own_im + mir_im
            copy = pltpu.make_async_copy(out_buf.at[s], out_ref.at[s], out_sem.at[s])
            copy.start()
            sent.append(copy)
        for copy in sent:
            copy.wait()


def walker_spec(width, offset, count):
    return pl.BlockSpec((1, 2, width, width), lambda w: (jnp.clip(w - offset, 0, count - 1), 0, 0, 0))


def accumulate(walkers, info, prior, final, slots, width, scale):
    has_prior = prior is not None
    counts = tuple(g.shape[0] for g in walkers)
    kernel = functools.partial(
        accumulate_kernel, slots=slots, width=width, scale=scale, has_prior=has_prior, final=final, counts=counts
    )
    full = lambda shape: pl.BlockSpec(shape, lambda w: (0,) * len(shape))
    acc_shape = (2 * slots, 2, width, width)
    out_shape = (slots, 2, width, width) if final else acc_shape
    ti, ph, far, slot, cj = info
    in_specs = [full(g.shape) for g in walkers] + [
        full(ti.shape),
        full(ph.shape),
        full(far.shape),
        pl.BlockSpec(memory_space=pltpu.SMEM),
        full(cj.shape),
    ]
    scratch = [pltpu.VMEM(acc_shape, F32), pltpu.VMEM((2 * slots * width, width), BF16)]
    operands = list(walkers) + [ti, ph, far, slot, cj]
    if has_prior:
        in_specs.append(pl.BlockSpec(memory_space=pl.ANY))
        scratch += [pltpu.VMEM(acc_shape, F32), pltpu.SemaphoreType.DMA(())]
        operands.append(prior)
    steps = sum(counts)
    flops = steps * 2 * slots * 8 * width**3 + (8 * slots * 2 * width**3 if final else 0)
    moved = sum(g.size for g in walkers) * 2 + 4 * math.prod(out_shape) + (4 * math.prod(acc_shape) if has_prior else 0)
    return pl.pallas_call(
        kernel,
        grid=(1,),
        cost_estimate=pl.CostEstimate(flops=flops, transcendentals=0, bytes_accessed=moved),
        in_specs=in_specs,
        out_specs=pl.BlockSpec(memory_space=pl.ANY),
        out_shape=jax.ShapeDtypeStruct(out_shape, F32),
        scratch_shapes=scratch + (
            [pltpu.VMEM(out_shape, F32), pltpu.SemaphoreType.DMA((slots,))]
            if final
            else [pltpu.SemaphoreType.DMA((2 * slots,))]
        ),
        compiler_params=pltpu.CompilerParams(dimension_semantics=("arbitrary",)),
    )(*operands)


def local(greens, transfer_index, phase_index, partner_slot, conj_index):
    slots = transfer_index.shape[0]
    width = greens.shape[-1]
    blocks = lax.axis_size("blk")
    halfway = lax.axis_size("xfer") // 2
    scale = 0.5 / math.sqrt(blocks)
    assert blocks % 2 == 0 and blocks & (blocks - 1) == 0 and 4 * slots + 1 <= 128

    swap = [(i, i ^ 1) for i in range(blocks)]
    sibling = lax.ppermute(greens, "blk", swap)
    fetched = [lax.ppermute(greens, "blk", [(i, i ^ (2 * m)) for i in range(blocks)]) for m in range(1, blocks // 2)]
    far = passed_along(jnp.concatenate([transfer_index, phase_index], axis=0), "xfer", halfway)
    info = (transfer_index, phase_index, far, partner_slot, conj_index.reshape(1, width))
    run = functools.partial(accumulate, info=info, slots=slots, width=width, scale=scale)

    if not fetched:
        return run([greens, sibling], prior=None, final=True)
    partial_sums = run([greens, sibling], prior=None, final=False)
    partial_sums, fetched = lax.optimization_barrier((partial_sums, [fetched[1]] + fetched[2:] + [fetched[0]]))
    near = jnp.concatenate(fetched, axis=0)
    forwarded = lax.ppermute(near, "blk", swap)
    partial_sums = run(fetched, prior=partial_sums, final=False)
    return run([forwarded], prior=partial_sums, final=True)


def solution(mesh):
    in_specs = (
        P("blk", None, None, None),
        P(("blk", "xfer"), None),
        P(("blk", "xfer"), None),
        P(("blk", "xfer")),
        P(),
    )
    out_specs = P(("blk", "xfer"), None, None, None)
    return jax.shard_map(local, mesh=mesh, in_specs=in_specs, out_specs=out_specs, check_vma=False)
```

```python
import functools
import math

import jax
import jax.numpy as jnp
from jax import lax
from jax.experimental import pallas as pl
from jax.experimental.pallas import tpu as pltpu
from jax.sharding import PartitionSpec as P

NPH = 8
F32 = jnp.float32
BF16 = jnp.bfloat16
NT = (((1,), (1,)), ((), ()))
CHUNK = 1
ROOT_HALF = math.sqrt(0.5)
COSINES = (1.0, ROOT_HALF, 0.0, -ROOT_HALF, -1.0, -ROOT_HALF, 0.0, ROOT_HALF)
SINES = (0.0, ROOT_HALF, 1.0, ROOT_HALF, 0.0, -ROOT_HALF, -1.0, -ROOT_HALF)


def passed_along(value, axis, by):
    size = lax.axis_size(axis)
    return lax.ppermute(value, axis, [(i, (i + by) % size) for i in range(size)])


def split2(x):
    hi = x.astype(BF16)
    return (hi, (x - hi.astype(F32)).astype(BF16))


def conj_permuted(q, x):
    total = None
    for piece in split2(x):
        rows = jnp.dot(q, piece, preferred_element_type=F32).astype(BF16)
        moved = lax.dot_general(q, rows, NT, preferred_element_type=F32)
        total = moved if total is None else total + moved
    return total


def table(levels, values):
    out = jnp.zeros(levels.shape, F32)
    for k, v in enumerate(values):
        out = jnp.where(levels == k, v, out)
    return out


def add_walkers(blocks, sel_ref, acc_ref, slots, width, finish=None):
    sel = sel_ref[...]
    terms = []
    for g_ref, k in blocks:
        g_re = g_ref[k, 0]
        g_im = g_ref[k, 1]
        y = jnp.dot(sel, jnp.concatenate([g_re, g_im], axis=1), preferred_element_type=F32).astype(BF16)
        terms.append((g_ref, k, y))
    for t in range(2 * slots):
        lo, hi = t * width, (t + 1) * width
        acc_re = acc_ref[t, 0]
        acc_im = acc_ref[t, 1]
        for g_ref, k, y in terms:
            gr = g_ref[k, 0].astype(F32)
            gi = g_ref[k, 1].astype(F32)
            stacked = jnp.concatenate([y[lo:hi, :width], y[lo:hi, width:]], axis=0)
            m = lax.dot_general(sel[lo:hi], stacked, NT, preferred_element_type=F32)
            m_re = m[:, :width]
            m_im = m[:, width:]
            acc_re = acc_re + (gr * m_re - gi * m_im)
            acc_im = acc_im + (gr * m_im + gi * m_re)
        if finish is None:
            acc_ref[t, 0] = acc_re
            acc_ref[t, 1] = acc_im
        else:
            finish(t, acc_re, acc_im)


def accumulate_kernel(*refs, slots, width, scale, has_prior, final, counts):
    groups = len(counts)
    g_refs = refs[:groups]
    refs = refs[groups:]
    if final:
        refs, out_buf, out_sem = refs[:-2], refs[-2], refs[-1]
    else:
        refs, out_sem = refs[:-1], refs[-1]
    if has_prior:
        (ti_ref, ph_ref, far_ref, slot_ref, cj_ref, prior_hbm, out_ref,
         acc_ref, sel_ref, prior_ref, sem) = refs
    else:
        ti_ref, ph_ref, far_ref, slot_ref, cj_ref, out_ref, acc_ref, sel_ref = refs
    w = pl.program_id(0)
    last = pl.num_programs(0) - 1
    nt = 2 * slots
    lanes = lax.broadcasted_iota(jnp.int32, (width, width), 1).astype(F32)

    def columns():
        far = far_ref[...]
        rows = [ti_ref[pl.ds(s, 1), :] for s in range(slots)]
        for s in range(slots):
            pick = slot_ref[s]
            rows.append(jnp.where(pick == 0, far[0:1], far[1:2]))
        rows.append(cj_ref[...])
        block = jnp.concatenate(rows, axis=0).astype(F32)
        block = jnp.concatenate([block, jnp.zeros((128 - block.shape[0], width), F32)], axis=0)
        return block.T

    @pl.when(w == 0)
    def _():
        acc_ref[...] = jnp.zeros(acc_ref.shape, F32)
        if has_prior:
            pltpu.make_async_copy(prior_hbm, prior_ref, sem).start()
        cols = columns()
        for t in range(nt):
            sel_ref[t * width:(t + 1) * width] = (cols[:, t:t + 1] == lanes).astype(BF16)

    out_copies = []

    def finish(t, acc_re, acc_im):
        if has_prior:
            if t == 0:
                pltpu.make_async_copy(prior_hbm, prior_ref, sem).wait()
            acc_re = acc_re + prior_ref[t, 0]
            acc_im = acc_im + prior_ref[t, 1]
        acc_ref[t, 0] = acc_re
        acc_ref[t, 1] = acc_im
        copy = pltpu.make_async_copy(acc_ref.at[t], out_ref.at[t], out_sem.at[t])
        copy.start()
        out_copies.append(copy)

    pending = [(g_ref, k) for g_ref, count in zip(g_refs, counts) for k in range(count)]
    starts = list(range(0, len(pending), CHUNK))
    for start in starts:
        hook = finish if (start == starts[-1] and not final) else None
        add_walkers(pending[start:start + CHUNK], sel_ref, acc_ref, slots, width, hook)
    for copy in out_copies:
        copy.wait()

    @pl.when(w == last)
    def _():
        if not final:
            return
        if has_prior:
            pltpu.make_async_copy(prior_hbm, prior_ref, sem).wait()
        cols = columns()
        q = (cols[:, nt:nt + 1] == lanes).astype(BF16)
        sent = []
        far = far_ref[...]
        partner = [jnp.where(slot_ref[s] == 0, far[2:3], far[3:4]) for s in range(slots)]
        partner = jnp.concatenate(partner + [jnp.zeros((8 - slots, width), jnp.int32)], axis=0)
        partner = lax.dot_general(partner.astype(F32).astype(BF16), q, NT, preferred_element_type=F32)
        levels = jnp.concatenate([ph_ref[...].astype(F32), partner[:slots]], axis=0)
        trig = jnp.concatenate([table(levels, COSINES), table(levels, SINES)], axis=0)
        trig_cols = jnp.concatenate([trig, jnp.zeros((128 - 2 * nt, width), F32)], axis=0).T
        for s in range(slots):
            parts = []
            for t, permute in ((s, False), (s + slots, True)):
                t_re = acc_ref[t, 0] + prior_ref[t, 0] if has_prior else acc_ref[t, 0]
                t_im = acc_ref[t, 1] + prior_ref[t, 1] if has_prior else acc_ref[t, 1]
                if permute:
                    t_re = conj_permuted(q, t_re)
                    t_im = -conj_permuted(q, t_im)
                ca = trig_cols[:, t:t + 1] * scale
                sa = trig_cols[:, nt + t:nt + t + 1] * scale
                cb = trig[t:t + 1]
                sb = trig[nt + t:nt + t + 1]
                rot_re = ca * cb + sa * sb
                rot_im = sa * cb - ca * sb
                parts.append((rot_re * t_re - rot_im * t_im, rot_re * t_im + rot_im * t_re))
            (own_re, own_im), (mir_re, mir_im) = parts
            out_buf[s, 0] = own_re + mir_re
            out_buf[s, 1] = own_im + mir_im
            copy = pltpu.make_async_copy(out_buf.at[s], out_ref.at[s], out_sem.at[s])
            copy.start()
            sent.append(copy)
        for copy in sent:
            copy.wait()


def walker_spec(width, offset, count):
    return pl.BlockSpec((1, 2, width, width), lambda w: (jnp.clip(w - offset, 0, count - 1), 0, 0, 0))


def accumulate(walkers, info, prior, final, slots, width, scale):
    has_prior = prior is not None
    counts = tuple(g.shape[0] for g in walkers)
    kernel = functools.partial(
        accumulate_kernel, slots=slots, width=width, scale=scale, has_prior=has_prior, final=final, counts=counts
    )
    full = lambda shape: pl.BlockSpec(shape, lambda w: (0,) * len(shape))
    acc_shape = (2 * slots, 2, width, width)
    out_shape = (slots, 2, width, width) if final else acc_shape
    ti, ph, far, slot, cj = info
    in_specs = [full(g.shape) for g in walkers] + [
        full(ti.shape),
        full(ph.shape),
        full(far.shape),
        pl.BlockSpec(memory_space=pltpu.SMEM),
        full(cj.shape),
    ]
    scratch = [pltpu.VMEM(acc_shape, F32), pltpu.VMEM((2 * slots * width, width), BF16)]
    operands = list(walkers) + [ti, ph, far, slot, cj]
    if has_prior:
        in_specs.append(pl.BlockSpec(memory_space=pl.ANY))
        scratch += [pltpu.VMEM(acc_shape, F32), pltpu.SemaphoreType.DMA(())]
        operands.append(prior)
    steps = sum(counts)
    flops = steps * 2 * slots * 8 * width**3 + (8 * slots * 2 * width**3 if final else 0)
    moved = sum(g.size for g in walkers) * 2 + 4 * math.prod(out_shape) + (4 * math.prod(acc_shape) if has_prior else 0)
    return pl.pallas_call(
        kernel,
        grid=(1,),
        cost_estimate=pl.CostEstimate(flops=flops, transcendentals=0, bytes_accessed=moved),
        in_specs=in_specs,
        out_specs=pl.BlockSpec(memory_space=pl.ANY),
        out_shape=jax.ShapeDtypeStruct(out_shape, F32),
        scratch_shapes=scratch + (
            [pltpu.VMEM(out_shape, F32), pltpu.SemaphoreType.DMA((slots,))]
            if final
            else [pltpu.SemaphoreType.DMA((2 * slots,))]
        ),
        compiler_params=pltpu.CompilerParams(dimension_semantics=("arbitrary",)),
    )(*operands)


def local(greens, transfer_index, phase_index, partner_slot, conj_index):
    slots = transfer_index.shape[0]
    width = greens.shape[-1]
    blocks = lax.axis_size("blk")
    halfway = lax.axis_size("xfer") // 2
    scale = 0.5 / math.sqrt(blocks)
    assert blocks % 2 == 0 and blocks & (blocks - 1) == 0 and 4 * slots + 1 <= 128

    swap = [(i, i ^ 1) for i in range(blocks)]
    sibling = lax.ppermute(greens, "blk", swap)
    fetched = [lax.ppermute(greens, "blk", [(i, i ^ (2 * m)) for i in range(blocks)]) for m in range(1, blocks // 2)]
    far = passed_along(jnp.concatenate([transfer_index, phase_index], axis=0), "xfer", halfway)
    info = (transfer_index, phase_index, far, partner_slot, conj_index.reshape(1, width))
    run = functools.partial(accumulate, info=info, slots=slots, width=width, scale=scale)

    if not fetched:
        return run([greens, sibling], prior=None, final=True)
    partial_sums = run([greens, sibling], prior=None, final=False)
    partial_sums, fetched = lax.optimization_barrier((partial_sums, [fetched[1], fetched[0]] + fetched[2:]))
    near = jnp.concatenate(fetched, axis=0)
    forwarded = lax.ppermute(near, "blk", swap)
    partial_sums = run(fetched, prior=partial_sums, final=False)
    return run([forwarded], prior=partial_sums, final=True)


def solution(mesh):
    in_specs = (
        P("blk", None, None, None),
        P(("blk", "xfer"), None),
        P(("blk", "xfer"), None),
        P(("blk", "xfer")),
        P(),
    )
    out_specs = P(("blk", "xfer"), None, None, None)
    return jax.shard_map(local, mesh=mesh, in_specs=in_specs, out_specs=out_specs, check_vma=False)
```

```python
import functools
import math

import jax
import jax.numpy as jnp
from jax import lax
from jax.experimental import pallas as pl
from jax.experimental.pallas import tpu as pltpu
from jax.sharding import PartitionSpec as P

NPH = 8
F32 = jnp.float32
BF16 = jnp.bfloat16
NT = (((1,), (1,)), ((), ()))
CHUNK = 1
ROOT_HALF = math.sqrt(0.5)
COSINES = (1.0, ROOT_HALF, 0.0, -ROOT_HALF, -1.0, -ROOT_HALF, 0.0, ROOT_HALF)
SINES = (0.0, ROOT_HALF, 1.0, ROOT_HALF, 0.0, -ROOT_HALF, -1.0, -ROOT_HALF)


def passed_along(value, axis, by):
    size = lax.axis_size(axis)
    return lax.ppermute(value, axis, [(i, (i + by) % size) for i in range(size)])


def split2(x):
    hi = x.astype(BF16)
    return (hi, (x - hi.astype(F32)).astype(BF16))


def conj_permuted(q, x):
    total = None
    for piece in split2(x):
        rows = jnp.dot(q, piece, preferred_element_type=F32).astype(BF16)
        moved = lax.dot_general(q, rows, NT, preferred_element_type=F32)
        total = moved if total is None else total + moved
    return total


def table(levels, values):
    out = jnp.zeros(levels.shape, F32)
    for k, v in enumerate(values):
        out = jnp.where(levels == k, v, out)
    return out


def add_walkers(blocks, sel_ref, acc_ref, slots, width, finish=None):
    sel = sel_ref[0:2 * slots * width]
    terms = []
    for g_ref, k in blocks:
        g_re = g_ref[k, 0]
        g_im = g_ref[k, 1]
        y = jnp.dot(sel, jnp.concatenate([g_re, g_im], axis=1), preferred_element_type=F32).astype(BF16)
        terms.append((g_re.astype(F32), g_im.astype(F32), y))
    for t in range(2 * slots):
        lo, hi = t * width, (t + 1) * width
        acc_re = acc_ref[t, 0]
        acc_im = acc_ref[t, 1]
        for gr, gi, y in terms:
            stacked = jnp.concatenate([y[lo:hi, :width], y[lo:hi, width:]], axis=0)
            m = lax.dot_general(sel[lo:hi], stacked, NT, preferred_element_type=F32)
            m_re = m[:, :width]
            m_im = m[:, width:]
            acc_re = acc_re + (gr * m_re - gi * m_im)
            acc_im = acc_im + (gr * m_im + gi * m_re)
        if finish is None:
            acc_ref[t, 0] = acc_re
            acc_ref[t, 1] = acc_im
        else:
            finish(t, acc_re, acc_im)


def accumulate_kernel(*refs, slots, width, scale, has_prior, final, counts):
    groups = len(counts)
    g_refs = refs[:groups]
    refs = refs[groups:]
    if final:
        refs, out_buf, out_sem = refs[:-2], refs[-2], refs[-1]
    else:
        refs, out_sem = refs[:-1], refs[-1]
    if has_prior:
        (ti_ref, ph_ref, far_ref, slot_ref, cj_ref, prior_hbm, out_ref,
         acc_ref, sel_ref, prior_ref, sem) = refs
    else:
        ti_ref, ph_ref, far_ref, slot_ref, cj_ref, out_ref, acc_ref, sel_ref = refs
    w = pl.program_id(0)
    last = pl.num_programs(0) - 1
    nt = 2 * slots
    lanes = lax.broadcasted_iota(jnp.int32, (width, width), 1).astype(F32)

    def columns():
        far = far_ref[...]
        rows = [ti_ref[pl.ds(s, 1), :] for s in range(slots)]
        for s in range(slots):
            pick = slot_ref[s]
            rows.append(jnp.where(pick == 0, far[0:1], far[1:2]))
        rows.append(cj_ref[...])
        block = jnp.concatenate(rows, axis=0).astype(F32)
        block = jnp.concatenate([block, jnp.zeros((128 - block.shape[0], width), F32)], axis=0)
        return block.T

    @pl.when(w == 0)
    def _():
        acc_ref[...] = jnp.zeros(acc_ref.shape, F32)
        if has_prior:
            pltpu.make_async_copy(prior_hbm, prior_ref, sem).start()
        cols = columns()
        for t in range(nt):
            sel_ref[t * width:(t + 1) * width] = (cols[:, t:t + 1] == lanes).astype(BF16)
        if final:
            sel_ref[nt * width:(nt + 1) * width] = (cols[:, nt:nt + 1] == lanes).astype(BF16)

    out_copies = []

    def finish(t, acc_re, acc_im):
        if has_prior:
            if t == 0:
                pltpu.make_async_copy(prior_hbm, prior_ref, sem).wait()
            acc_re = acc_re + prior_ref[t, 0]
            acc_im = acc_im + prior_ref[t, 1]
        acc_ref[t, 0] = acc_re
        acc_ref[t, 1] = acc_im
        copy = pltpu.make_async_copy(acc_ref.at[t], out_ref.at[t], out_sem.at[t])
        copy.start()
        out_copies.append(copy)

    pending = [(g_ref, k) for g_ref, count in zip(g_refs, counts) for k in range(count)]
    starts = list(range(0, len(pending), CHUNK))
    for start in starts:
        hook = finish if (start == starts[-1] and not final) else None
        add_walkers(pending[start:start + CHUNK], sel_ref, acc_ref, slots, width, hook)
    for copy in out_copies:
        copy.wait()

    @pl.when(w == last)
    def _():
        if not final:
            return
        if has_prior:
            pltpu.make_async_copy(prior_hbm, prior_ref, sem).wait()
        q = sel_ref[nt * width:(nt + 1) * width]
        sent = []
        far = far_ref[...]
        partner = [jnp.where(slot_ref[s] == 0, far[2:3], far[3:4]) for s in range(slots)]
        partner = jnp.concatenate(partner + [jnp.zeros((8 - slots, width), jnp.int32)], axis=0)
        partner = lax.dot_general(partner.astype(F32).astype(BF16), q, NT, preferred_element_type=F32)
        levels = jnp.concatenate([ph_ref[...].astype(F32), partner[:slots]], axis=0)
        trig = jnp.concatenate([table(levels, COSINES), table(levels, SINES)], axis=0)
        trig_cols = jnp.concatenate([trig, jnp.zeros((128 - 2 * nt, width), F32)], axis=0).T
        for s in range(slots):
            parts = []
            for t, permute in ((s, False), (s + slots, True)):
                t_re = acc_ref[t, 0] + prior_ref[t, 0] if has_prior else acc_ref[t, 0]
                t_im = acc_ref[t, 1] + prior_ref[t, 1] if has_prior else acc_ref[t, 1]
                if permute:
                    t_re = conj_permuted(q, t_re)
                    t_im = -conj_permuted(q, t_im)
                ca = trig_cols[:, t:t + 1] * scale
                sa = trig_cols[:, nt + t:nt + t + 1] * scale
                cb = trig[t:t + 1]
                sb = trig[nt + t:nt + t + 1]
                rot_re = ca * cb + sa * sb
                rot_im = sa * cb - ca * sb
                parts.append((rot_re * t_re - rot_im * t_im, rot_re * t_im + rot_im * t_re))
            (own_re, own_im), (mir_re, mir_im) = parts
            out_buf[s, 0] = own_re + mir_re
            out_buf[s, 1] = own_im + mir_im
            copy = pltpu.make_async_copy(out_buf.at[s], out_ref.at[s], out_sem.at[s])
            copy.start()
            sent.append(copy)
        for copy in sent:
            copy.wait()


def walker_spec(width, offset, count):
    return pl.BlockSpec((1, 2, width, width), lambda w: (jnp.clip(w - offset, 0, count - 1), 0, 0, 0))


def accumulate(walkers, info, prior, final, slots, width, scale):
    has_prior = prior is not None
    counts = tuple(g.shape[0] for g in walkers)
    kernel = functools.partial(
        accumulate_kernel, slots=slots, width=width, scale=scale, has_prior=has_prior, final=final, counts=counts
    )
    full = lambda shape: pl.BlockSpec(shape, lambda w: (0,) * len(shape))
    acc_shape = (2 * slots, 2, width, width)
    out_shape = (slots, 2, width, width) if final else acc_shape
    ti, ph, far, slot, cj = info
    in_specs = [full(g.shape) for g in walkers] + [
        full(ti.shape),
        full(ph.shape),
        full(far.shape),
        pl.BlockSpec(memory_space=pltpu.SMEM),
        full(cj.shape),
    ]
    scratch = [pltpu.VMEM(acc_shape, F32), pltpu.VMEM(((2 * slots + 1) * width, width), BF16)]
    operands = list(walkers) + [ti, ph, far, slot, cj]
    if has_prior:
        in_specs.append(pl.BlockSpec(memory_space=pl.ANY))
        scratch += [pltpu.VMEM(acc_shape, F32), pltpu.SemaphoreType.DMA(())]
        operands.append(prior)
    steps = sum(counts)
    flops = steps * 2 * slots * 8 * width**3 + (8 * slots * 2 * width**3 if final else 0)
    moved = sum(g.size for g in walkers) * 2 + 4 * math.prod(out_shape) + (4 * math.prod(acc_shape) if has_prior else 0)
    return pl.pallas_call(
        kernel,
        grid=(1,),
        cost_estimate=pl.CostEstimate(flops=flops, transcendentals=0, bytes_accessed=moved),
        in_specs=in_specs,
        out_specs=pl.BlockSpec(memory_space=pl.ANY),
        out_shape=jax.ShapeDtypeStruct(out_shape, F32),
        scratch_shapes=scratch + (
            [pltpu.VMEM(out_shape, F32), pltpu.SemaphoreType.DMA((slots,))]
            if final
            else [pltpu.SemaphoreType.DMA((2 * slots,))]
        ),
        compiler_params=pltpu.CompilerParams(dimension_semantics=("arbitrary",)),
    )(*operands)


def local(greens, transfer_index, phase_index, partner_slot, conj_index):
    slots = transfer_index.shape[0]
    width = greens.shape[-1]
    blocks = lax.axis_size("blk")
    halfway = lax.axis_size("xfer") // 2
    scale = 0.5 / math.sqrt(blocks)
    assert blocks % 2 == 0 and blocks & (blocks - 1) == 0 and 4 * slots + 1 <= 128

    swap = [(i, i ^ 1) for i in range(blocks)]
    sibling = lax.ppermute(greens, "blk", swap)
    fetched = [lax.ppermute(greens, "blk", [(i, i ^ (2 * m)) for i in range(blocks)]) for m in range(1, blocks // 2)]
    far = passed_along(jnp.concatenate([transfer_index, phase_index], axis=0), "xfer", halfway)
    info = (transfer_index, phase_index, far, partner_slot, conj_index.reshape(1, width))
    run = functools.partial(accumulate, info=info, slots=slots, width=width, scale=scale)

    if not fetched:
        return run([greens, sibling], prior=None, final=True)
    partial_sums = run([greens, sibling], prior=None, final=False)
    partial_sums, fetched = lax.optimization_barrier((partial_sums, [fetched[1], fetched[0]] + fetched[2:]))
    near = jnp.concatenate(fetched, axis=0)
    forwarded = lax.ppermute(near, "blk", swap)
    partial_sums = run(fetched, prior=partial_sums, final=False)
    return run([forwarded], prior=partial_sums, final=True)


def solution(mesh):
    in_specs = (
        P("blk", None, None, None),
        P(("blk", "xfer"), None),
        P(("blk", "xfer"), None),
        P(("blk", "xfer")),
        P(),
    )
    out_specs = P(("blk", "xfer"), None, None, None)
    return jax.shard_map(local, mesh=mesh, in_specs=in_specs, out_specs=out_specs, check_vma=False)
```
